128 devices in a mesh: gx: 16 (over z, y_hi, core), gy: 8 (over y_lo, x).
Axes of the slice: x: 4, y: 4 (y_hi: 2, y_lo: 2; y = y_hi * 2 + y_lo), z: 4, core: 2. Of those that a mesh axis runs over, the one named last changes fastest.
Arguments:
- velocity: float32 [3, 128, 64, 256], P(None, 'gy', 'gx'), may hold values from -6 to 6
- point_velocity: float32 [3, 16384], P(None, ('gx', 'gy')), may hold values from -8 to 8
- point_coef: float32 [16384], P(('gx', 'gy')), may hold values from 0.05 to 0.5
- point_width: float32 [16384], P(('gx', 'gy')), may hold values from 0.8 to 2
- send_point: int32 [128, 2048], P(('gx', 'gy')), may hold values from 0 to 127
- send_count: int32 [128, 128], P(('gx', 'gy')), may hold values from 0 to 16, as said below
- slot_offset: float32 [3, 128, 2048], P(None, ('gx', 'gy')), may hold values from 0.5 to 3.5
- send_anchor: int32 [128, 2048], P(('gx', 'gy')), may hold values from 0 to 12540, as said below
- vertical_inverse: float32 [64, 64], replicated, may hold values from -1 to 2, as said below
Outputs:
- new_velocity: float32 [3, 128, 64, 256], P(None, 'gy', 'gx')
The draws below stay inside these ranges and needn't reach their ends.
Inputs may be any that keep to these rules, and one draw needn't show every extreme that they name: `send_count`: one destination tile, drawn from the seed, has 16 records from every source device. `send_anchor`: every block of 4 x 4 x 4 cells at the corner lies inside the destination tile: the corner is x * 4 * 256 + z * 256 + y with x <= 12, z <= 0, y <= 252. `vertical_inverse`: a dense matrix.
All inputs are finite; a program needn't handle non-finite values.
Results may differ from the reference program's by a relative error of at most 0.00007.
Values sent between devices are 32-bit elements; how exact they have to be, the bound alone decides.
No kernel may reach another device: no remote copies, remote signals or barrier semaphores. Data moves between devices by JAX's collectives and lax.ppermute only.
A program may use at most 64 MiB of HBM per device.

```python
import math
import jax
import jax.numpy as jnp
from jax import lax

CX = 16
CZ = 4
NY = 256
PTS_DEV = 128
CAP = 16
K = 4
NDEV = 128
NX = 128
NZ = 64
N_GY = 8


def draw_send_count(key, part):
    key_busy, key_many, key_few, key_full = jax.random.split(key, 4)
    busy_dest = jax.random.randint(key_busy, (NDEV,), 0, 4) == 0
    many_rows = jax.random.randint(key_many, (NDEV, NDEV), 0, CAP + 1)
    few_rows = jnp.minimum(jax.random.randint(key_few, (NDEV, NDEV), 0, 3), CAP)
    counts_table = jnp.where(busy_dest[None, :], many_rows, few_rows)
    full_dest = jax.random.randint(key_full, (), 0, NDEV)
    full_column = jnp.arange(NDEV) == full_dest
    return jnp.where(full_column[None, :], CAP, counts_table).astype(jnp.int32)


def draw_send_anchor(key, part):
    key_x, key_z, key_y, key_low, key_high = jax.random.split(jax.random.fold_in(key, 7), 5)
    table_shape = (NDEV, NDEV * CAP)
    corner_x = jax.random.randint(key_x, table_shape, 0, CX - K + 1)
    corner_z = jax.random.randint(key_z, table_shape, 0, CZ - K + 1)
    corner_y = jax.random.randint(key_y, table_shape, 0, NY - K + 1)
    anchors = corner_x * (CZ * NY) + corner_z * NY + corner_y
    flat_index = jnp.arange(NDEV * NDEV * CAP).reshape(table_shape)
    low_spot = jax.random.randint(key_low, (), 0, NDEV * NDEV * CAP // 2)
    high_spot = jax.random.randint(key_high, (), NDEV * NDEV * CAP // 2, NDEV * NDEV * CAP)
    top_value = (CX - K) * (CZ * NY) + (CZ - K) * NY + (NY - K)
    anchors = jnp.where(flat_index == low_spot, 0, anchors)
    anchors = jnp.where(flat_index == high_spot, top_value, anchors)
    return anchors.astype(jnp.int32)


def draw_vertical_inverse(key, part):
    key_spread, key_diag = jax.random.split(jax.random.fold_in(key, 11), 2)
    row_index = jnp.arange(NZ)[:, None]
    col_index = jnp.arange(NZ)[None, :]
    distance = jnp.abs(row_index - col_index).astype(jnp.float32)
    spread = jax.random.uniform(key_spread, (NZ, NZ), minval=0.2, maxval=1.0)
    diagonal = jax.random.uniform(key_diag, (NZ,), minval=1.0, maxval=2.0)
    falloff = jnp.exp(-distance / (NZ / 4.0))
    identity_mask = (row_index == col_index).astype(jnp.float32)
    off_part = spread * falloff * (3.0 / NZ)
    return (off_part * (1.0 - identity_mask) + identity_mask * diagonal[:, None]).astype(jnp.float32)


def plant(drawn, rng, least, high):
    place = [jax.random.randint(jax.random.fold_in(rng, axis), (), 0, length) for axis, length in enumerate(drawn.shape)]
    longest = drawn.shape.index(max(drawn.shape))
    beside = place[:longest] + [(place[longest] + 1) % drawn.shape[longest]] + place[longest + 1:]
    return drawn.at[tuple(place)].set(least).at[tuple(beside)].set(high)


def block_scale(own_key, dims, shards, smallest, largest):
    def one(axis_at, blocks):
        draws = jax.random.uniform(jax.random.fold_in(jax.random.fold_in(own_key, 6), axis_at), (blocks,), jnp.float32, smallest / len(shards), largest / len(shards))
        return jnp.repeat(jnp.exp(draws), dims[axis_at] // blocks).reshape((-1,) + (1,) * (len(dims) - axis_at - 1))

    level = one(*shards[0])
    for cut in shards[1:]:
        level = level * one(*cut)
    return level


def noise(own_key, extent, width, bound, cuts=(), kind=jnp.bfloat16):
    values = width * jax.random.normal(own_key, extent, jnp.float32)
    if cuts:
        values = values * block_scale(own_key, extent, cuts, -0.22, 0.18)
    return jnp.clip(values, -bound, bound).astype(kind)


def setup_inputs(seed: int = 0) -> dict:
    streams_of = jax.random.split(jax.random.key(seed), 10)
    velocity = noise(streams_of[0], (3, NX, NZ, NY), 1.0, 6.0, ((1, 8), (2, 16)), jnp.float32)
    point_velocity = noise(streams_of[1], (3, NDEV * PTS_DEV), 2.0, 8.0, ((1, 128),), jnp.float32)
    point_coef = jnp.clip(jnp.exp(math.log(0.5) - 2.3025851 * jax.random.uniform(streams_of[2], (NDEV * PTS_DEV,), jnp.float32) ** block_scale(streams_of[2], (NDEV * PTS_DEV,), ((0, 128),), -0.2, 0.2)), 0.05, 0.5)
    point_width = jnp.clip(jnp.exp(math.log(2.0) - 0.9162907 * jax.random.uniform(streams_of[3], (NDEV * PTS_DEV,), jnp.float32) ** block_scale(streams_of[3], (NDEV * PTS_DEV,), ((0, 128),), -0.2, 0.2)), 0.8, 2.0)
    send_point = plant(jax.random.randint(streams_of[4], (NDEV, NDEV * CAP), 0, PTS_DEV), jax.random.fold_in(streams_of[4], 1), 0, PTS_DEV - 1).astype(jnp.int32)
    send_count = draw_send_count(jax.random.fold_in(streams_of[9], 71), 0)
    slot_offset = jnp.clip(0.5 + 3.0 * jax.random.uniform(streams_of[6], (3, NDEV, NDEV * CAP), jnp.float32) ** block_scale(streams_of[6], (3, NDEV, NDEV * CAP), ((1, 128),), -0.2, 0.2), 0.5, 3.5)
    send_anchor = draw_send_anchor(jax.random.fold_in(streams_of[9], 71), 0)
    vertical_inverse = draw_vertical_inverse(jax.random.fold_in(streams_of[9], 71), 0)
    return {"velocity": velocity, "point_velocity": point_velocity, "point_coef": point_coef, "point_width": point_width, "send_point": send_point, "send_count": send_count, "slot_offset": slot_offset, "send_anchor": send_anchor, "vertical_inverse": vertical_inverse}


time_step = 0.25

def spread_forces(records, corner_x, corner_z, corner_y, extent_z, extent_y, total_cells, block_edge):
    steps_range = jnp.arange(block_edge, dtype=jnp.int32)
    shift_x = jnp.repeat(steps_range, block_edge * block_edge)
    shift_z = jnp.tile(jnp.repeat(steps_range, block_edge), block_edge)
    shift_y = jnp.tile(steps_range, block_edge * block_edge)
    centre_x = shift_x.astype(jnp.float32) + 0.5
    centre_z = shift_z.astype(jnp.float32) + 0.5
    centre_y = shift_y.astype(jnp.float32) + 0.5
    distance = (centre_x[:, None] - records[3][None, :]) ** 2
    distance = distance + (centre_z[:, None] - records[4][None, :]) ** 2
    distance = distance + (centre_y[:, None] - records[5][None, :]) ** 2
    kernel_width = records[6][None, :]
    weight = jnp.exp(-distance / (kernel_width * kernel_width)) / (math.pi ** 1.5 * kernel_width ** 3)
    cell_index = (corner_x[None, :] + shift_x[:, None]) * (extent_z * extent_y)
    cell_index = cell_index + (corner_z[None, :] + shift_z[:, None]) * extent_y
    cell_index = (cell_index + corner_y[None, :] + shift_y[:, None]).astype(jnp.int32)
    deposits = records[0:3, None, :] * weight[None, :, :]
    deposit_field = jnp.zeros((3, total_cells), jnp.float32)
    return deposit_field.at[:, cell_index.reshape(-1)].add(deposits.reshape(3, -1))

def advect(velocity):
    grad_x = (jnp.roll(velocity, -1, axis=1) - jnp.roll(velocity, 1, axis=1)) * 0.5
    padded = jnp.pad(velocity, ((0, 0), (0, 0), (1, 1), (0, 0)))
    grad_z = (padded[:, :, 2:] - padded[:, :, :-2]) * 0.5
    grad_y = (jnp.roll(velocity, -1, axis=3) - jnp.roll(velocity, 1, axis=3)) * 0.5
    return velocity[0:1] * grad_x + velocity[1:2] * grad_y + velocity[2:3] * grad_z

def reference(velocity, point_velocity, point_coef, point_width, send_point, send_count, slot_offset, send_anchor, vertical_inverse):
    slot_total = NDEV * CAP
    point_speed = jnp.sqrt(lax.optimization_barrier(jnp.sum(point_velocity * point_velocity, axis=0)))
    point_force = -(point_coef * point_speed)[None, :] * point_velocity
    owner_base = (jnp.arange(NDEV, dtype=jnp.int32) * PTS_DEV)[:, None]
    chosen = (send_point + owner_base).reshape(-1).astype(jnp.int32)
    limits = jnp.repeat(send_count, CAP, axis=1)
    within = ((jnp.arange(slot_total, dtype=jnp.int32) % CAP)[None, :] < limits).reshape(-1)
    slot_force = jnp.take(point_force, chosen, axis=1) * within.astype(jnp.float32)[None, :]
    slot_width = jnp.take(point_width, chosen)[None, :]
    records = jnp.concatenate([slot_force, slot_offset.reshape(3, -1), slot_width], axis=0)
    anchors = send_anchor.reshape(NDEV, NDEV, CAP).transpose(1, 0, 2).reshape(-1).astype(jnp.int32)
    local_x = anchors // (CZ * NY)
    remainder = anchors % (CZ * NY)
    local_z = remainder // NY
    local_y = remainder % NY
    target = jnp.tile(jnp.repeat(jnp.arange(NDEV, dtype=jnp.int32), CAP), NDEV)
    corner_x = target % N_GY * CX + local_x
    corner_z = target // N_GY * CZ + local_z
    forcing = spread_forces(records, corner_x, corner_z, local_y, NZ, NY, NX * NZ * NY, K).reshape(3, NX, NZ, NY)
    transport = advect(velocity)
    updated = velocity + time_step * (forcing - transport)
    return jnp.einsum('zk,cxky->cxzy', vertical_inverse, updated, precision=lax.Precision.HIGHEST)
```

```python
import math

import jax
import jax.numpy as jnp
from jax import lax
from jax.sharding import PartitionSpec as P

K = 4


time_step = 0.25


def with_halo(block, sides, width, periodic):
    for axis, dim in sides:
        count = lax.axis_size(axis)
        forward = [(i, i + 1) for i in range(count - 1)]
        if periodic:
            forward.append((count - 1, 0))
        backward = [(target, source) for source, target in forward]
        low = lax.ppermute(
            lax.slice_in_dim(block, block.shape[dim] - width, None, axis=dim), axis, forward
        )
        high = lax.ppermute(lax.slice_in_dim(block, 0, width, axis=dim), axis, backward)
        block = jnp.concatenate([low, block, high], axis=dim)
    return block


def block_factor(corner, offset, extent, inverse_square, block_edge):
    cells = jnp.arange(extent, dtype=jnp.int32)[:, None]
    shifted = cells - corner[None, :]
    inside = (shifted >= 0) & (shifted < block_edge)
    spread = shifted.astype(jnp.float32) + 0.5 - offset[None, :]
    return jnp.where(inside, jnp.exp(-(spread * spread) * inverse_square[None, :]), 0.0)


def deposit_blocks(arrived, corner_x, corner_z, corner_y, rows_x, rows_z, rows_y, block_edge):
    width = arrived[6]
    inverse_square = 1.0 / (width * width)
    scaled = arrived[0:3] / (math.pi**1.5 * width**3)[None, :]
    along_x = block_factor(corner_x, arrived[3], rows_x, inverse_square, block_edge)
    along_z = block_factor(corner_z, arrived[4], rows_z, inverse_square, block_edge)
    along_y = block_factor(corner_y, arrived[5], rows_y, inverse_square, block_edge)
    left = scaled[:, None, None, :] * along_x[None, :, None, :] * along_z[None, None, :, :]
    left = left.reshape(3 * rows_x * rows_z, -1)
    result = lax.dot_general(
        left,
        along_y,
        (((1,), (1,)), ((), ())),
        precision=lax.Precision.HIGHEST,
        preferred_element_type=jnp.float32,
    )
    return result.reshape(3, rows_x, rows_z, rows_y)


def local(
    velocity,
    point_velocity,
    point_coef,
    point_width,
    send_point,
    send_count,
    slot_offset,
    send_anchor,
    vertical_inverse,
):
    rows_x = velocity.shape[1]
    rows_z = velocity.shape[2]
    rows_y = velocity.shape[3]
    slot_total = send_point.shape[1]
    device_count = lax.axis_size("gx") * lax.axis_size("gy")
    capacity = slot_total // device_count
    point_speed = jnp.sqrt(jnp.sum(point_velocity * point_velocity, axis=0))
    point_force = -(point_coef * point_speed)[None, :] * point_velocity
    chosen = send_point[0]
    limits = jnp.repeat(send_count[0], capacity)
    within = jnp.arange(slot_total, dtype=jnp.int32) % capacity < limits
    point_count = point_velocity.shape[1]
    pick = (jnp.arange(point_count, dtype=jnp.int32)[:, None] == chosen[None, :]).astype(jnp.float32)
    point_values = jnp.concatenate([point_force, point_width[None, :]], axis=0)
    picked = jnp.dot(point_values, pick, precision=lax.Precision.HIGHEST, preferred_element_type=jnp.float32)
    slot_force = picked[0:3] * within.astype(jnp.float32)[None, :]
    slot_width = picked[3:4]
    records = jnp.concatenate([slot_force, slot_offset[:, 0, :], slot_width], axis=0)
    arrived = lax.all_to_all(records, ("gx", "gy"), split_axis=1, concat_axis=1, tiled=True)
    anchors = send_anchor[0]
    corner_x = anchors // (rows_z * rows_y)
    remainder = anchors % (rows_z * rows_y)
    corner_z = remainder // rows_y
    corner_y = remainder % rows_y
    forcing = deposit_blocks(arrived, corner_x, corner_z, corner_y, rows_x, rows_z, rows_y, K)
    wide_x = with_halo(velocity, (("gy", 1),), 1, True)
    wide_z = with_halo(velocity, (("gx", 2),), 1, False)
    grad_x = (wide_x[:, 2:] - wide_x[:, :-2]) * 0.5
    grad_z = (wide_z[:, :, 2:] - wide_z[:, :, :-2]) * 0.5
    grad_y = (jnp.roll(velocity, -1, axis=3) - jnp.roll(velocity, 1, axis=3)) * 0.5
    transport = velocity[0:1] * grad_x + velocity[1:2] * grad_y + velocity[2:3] * grad_z
    updated = velocity + time_step * (forcing - transport)
    columns = lax.all_to_all(updated, "gx", split_axis=1, concat_axis=2, tiled=True)
    solved = jnp.einsum("zk,cxky->cxzy", vertical_inverse, columns, precision=lax.Precision.HIGHEST)
    new_velocity = lax.all_to_all(solved, "gx", split_axis=2, concat_axis=1, tiled=True)
    return new_velocity


def solution(mesh):
    placed = (
        P(None, "gy", "gx", None),
        P(None, ("gx", "gy")),
        P(("gx", "gy")),
        P(("gx", "gy")),
        P(("gx", "gy"), None),
        P(("gx", "gy"), None),
        P(None, ("gx", "gy"), None),
        P(("gx", "gy"), None),
        P(),
    )
    return jax.shard_map(
        local, mesh=mesh, in_specs=placed, out_specs=P(None, "gy", "gx", None), check_vma=False
    )
```

```python
import math

import jax
import jax.numpy as jnp
from jax import lax
from jax.sharding import PartitionSpec as P

K = 4


time_step = 0.25


def with_halo(block, sides, width, periodic):
    for axis, dim in sides:
        count = lax.axis_size(axis)
        forward = [(i, i + 1) for i in range(count - 1)]
        if periodic:
            forward.append((count - 1, 0))
        backward = [(target, source) for source, target in forward]
        low = lax.ppermute(
            lax.slice_in_dim(block, block.shape[dim] - width, None, axis=dim), axis, forward
        )
        high = lax.ppermute(lax.slice_in_dim(block, 0, width, axis=dim), axis, backward)
        block = jnp.concatenate([low, block, high], axis=dim)
    return block


def block_factor(corner, offset, extent, inverse_square, block_edge):
    cells = jnp.arange(extent, dtype=jnp.int32)[:, None]
    shifted = cells - corner[None, :]
    inside = (shifted >= 0) & (shifted < block_edge)
    spread = shifted.astype(jnp.float32) + 0.5 - offset[None, :]
    return jnp.where(inside, jnp.exp(-(spread * spread) * inverse_square[None, :]), 0.0)


def deposit_blocks(arrived, corner_x, corner_z, corner_y, rows_x, rows_z, rows_y, block_edge):
    width = arrived[6]
    inverse_square = 1.0 / (width * width)
    scaled = arrived[0:3] / (math.pi**1.5 * width**3)[None, :]
    along_x = block_factor(corner_x, arrived[3], rows_x, inverse_square, block_edge)
    along_z = block_factor(corner_z, arrived[4], rows_z, inverse_square, block_edge)
    along_y = block_factor(corner_y, arrived[5], rows_y, inverse_square, block_edge)
    left = scaled[:, None, None, :] * along_x[None, :, None, :] * along_z[None, None, :, :]
    left = left.reshape(3 * rows_x * rows_z, -1)
    result = lax.dot_general(
        left,
        along_y,
        (((1,), (1,)), ((), ())),
        precision=lax.Precision.HIGHEST,
        preferred_element_type=jnp.float32,
    )
    return result.reshape(3, rows_x, rows_z, rows_y)


def local(
    velocity,
    point_velocity,
    point_coef,
    point_width,
    send_point,
    send_count,
    slot_offset,
    send_anchor,
    vertical_inverse,
):
    rows_x = velocity.shape[1]
    rows_z = velocity.shape[2]
    rows_y = velocity.shape[3]
    slot_total = send_point.shape[1]
    device_count = lax.axis_size("gx") * lax.axis_size("gy")
    capacity = slot_total // device_count
    point_speed = jnp.sqrt(jnp.sum(point_velocity * point_velocity, axis=0))
    point_force = -(point_coef * point_speed)[None, :] * point_velocity
    chosen = send_point[0]
    limits = jnp.repeat(send_count[0], capacity)
    within = jnp.arange(slot_total, dtype=jnp.int32) % capacity < limits
    point_count = point_velocity.shape[1]
    pick = (jnp.arange(point_count, dtype=jnp.int32)[:, None] == chosen[None, :]).astype(jnp.float32)
    point_values = jnp.concatenate([point_force, point_width[None, :]], axis=0)
    picked = jnp.dot(point_values, pick, precision=lax.Precision.HIGHEST, preferred_element_type=jnp.float32)
    slot_force = picked[0:3] * within.astype(jnp.float32)[None, :]
    slot_width = picked[3:4]
    spare = jnp.zeros_like(slot_width)
    records = jnp.concatenate([slot_force, slot_offset[:, 0, :], slot_width, spare], axis=0)
    fields = records.shape[0]
    records = records.reshape(fields, device_count, capacity).transpose(1, 0, 2)
    records = records.reshape(device_count, fields * capacity)
    arrived = lax.all_to_all(records, ("gx", "gy"), split_axis=0, concat_axis=0, tiled=True)
    arrived = arrived.reshape(device_count, fields, capacity).transpose(1, 0, 2)
    arrived = arrived.reshape(fields, slot_total)
    anchors = send_anchor[0]
    corner_x = anchors // (rows_z * rows_y)
    remainder = anchors % (rows_z * rows_y)
    corner_z = remainder // rows_y
    corner_y = remainder % rows_y
    forcing = deposit_blocks(arrived, corner_x, corner_z, corner_y, rows_x, rows_z, rows_y, K)
    wide_x = with_halo(velocity, (("gy", 1),), 1, True)
    wide_z = with_halo(velocity, (("gx", 2),), 1, False)
    grad_x = (wide_x[:, 2:] - wide_x[:, :-2]) * 0.5
    grad_z = (wide_z[:, :, 2:] - wide_z[:, :, :-2]) * 0.5
    grad_y = (jnp.roll(velocity, -1, axis=3) - jnp.roll(velocity, 1, axis=3)) * 0.5
    transport = velocity[0:1] * grad_x + velocity[1:2] * grad_y + velocity[2:3] * grad_z
    updated = velocity + time_step * (forcing - transport)
    columns = lax.all_to_all(updated, "gx", split_axis=1, concat_axis=2, tiled=True)
    solved = jnp.einsum("zk,cxky->cxzy", vertical_inverse, columns, precision=lax.Precision.HIGHEST)
    new_velocity = lax.all_to_all(solved, "gx", split_axis=2, concat_axis=1, tiled=True)
    return new_velocity


def solution(mesh):
    placed = (
        P(None, "gy", "gx", None),
        P(None, ("gx", "gy")),
        P(("gx", "gy")),
        P(("gx", "gy")),
        P(("gx", "gy"), None),
        P(("gx", "gy"), None),
        P(None, ("gx", "gy"), None),
        P(("gx", "gy"), None),
        P(),
    )
    return jax.shard_map(
        local, mesh=mesh, in_specs=placed, out_specs=P(None, "gy", "gx", None), check_vma=False
    )
```

```python
import math

import jax
import jax.numpy as jnp
from jax import lax
from jax.experimental import pallas as pl
from jax.sharding import PartitionSpec as P

HIGHEST = lax.Precision.HIGHEST


def _rows(pieces, shape):
    row = lax.broadcasted_iota(jnp.int32, shape, 0)
    total = jnp.zeros(shape, jnp.float32)
    for k, piece in enumerate(pieces):
        total = jnp.where(row == k, jnp.broadcast_to(piece, shape), total)
    return total


def source_kernel(pv_ref, coef_ref, width_ref, sp_ref, cnt_ref, off_ref, out_ref):
    points = pv_ref.shape[1]
    slots = sp_ref.shape[1]
    tiles = cnt_ref.shape[1]
    capacity = slots // tiles
    fields = out_ref.shape[1] // capacity
    pv = pv_ref[...]
    speed = jnp.sqrt(pv[0:1] * pv[0:1] + pv[1:2] * pv[1:2] + pv[2:3] * pv[2:3])
    force = -(coef_ref[...] * speed) * pv
    vals = _rows([force[0:1], force[1:2], force[2:3], width_ref[...]], (8, points))
    pick = (lax.broadcasted_iota(jnp.int32, (points, slots), 0) == sp_ref[...]).astype(jnp.float32)
    picked = jnp.dot(vals, pick, precision=HIGHEST, preferred_element_type=jnp.float32)
    slot_at = lax.broadcasted_iota(jnp.int32, (tiles, slots), 1)
    tile_at = lax.broadcasted_iota(jnp.int32, (tiles, slots), 0)
    tile_of = (slot_at // capacity == tile_at).astype(jnp.float32)
    counts = _rows([cnt_ref[...].astype(jnp.float32)], (8, tiles))
    limit = jnp.dot(counts, tile_of, precision=HIGHEST, preferred_element_type=jnp.float32)[0:1]
    lane = (lax.broadcasted_iota(jnp.int32, (1, slots), 1) % capacity).astype(jnp.float32)
    live = jnp.where(lane < limit, 1.0, 0.0)
    off = off_ref[...]
    table = _rows([picked[0:1] * live, picked[1:2] * live, picked[2:3] * live,
                   off[0:1], off[1:2], off[2:3], picked[3:4]], (fields, slots))
    lanes_out = fields * capacity
    field_of = (lax.broadcasted_iota(jnp.int32, (lanes_out, fields), 0) // capacity
                == lax.broadcasted_iota(jnp.int32, (lanes_out, fields), 1)).astype(jnp.float32)
    spread = jnp.dot(field_of, table, precision=HIGHEST, preferred_element_type=jnp.float32)
    same_c = (lax.broadcasted_iota(jnp.int32, (lanes_out, slots), 1) % capacity
              == lax.broadcasted_iota(jnp.int32, (lanes_out, slots), 0) % capacity)
    spread = jnp.where(same_c, spread, 0.0)
    out_ref[...] = lax.dot_general(tile_of, spread, (((1,), (1,)), ((), ())), precision=HIGHEST,
                                   preferred_element_type=jnp.float32)


def source_records(pv, coef, width, sp, cnt, off):
    tiles = cnt.shape[1]
    capacity = sp.shape[1] // tiles
    return pl.pallas_call(
        source_kernel,
        out_shape=jax.ShapeDtypeStruct((tiles, 8 * capacity), jnp.float32),
    )(pv, coef, width, sp, cnt, off)

K = 4


time_step = 0.25


def with_halo(block, sides, width, periodic):
    for axis, dim in sides:
        count = lax.axis_size(axis)
        forward = [(i, i + 1) for i in range(count - 1)]
        if periodic:
            forward.append((count - 1, 0))
        backward = [(target, source) for source, target in forward]
        low = lax.ppermute(
            lax.slice_in_dim(block, block.shape[dim] - width, None, axis=dim), axis, forward
        )
        high = lax.ppermute(lax.slice_in_dim(block, 0, width, axis=dim), axis, backward)
        block = jnp.concatenate([low, block, high], axis=dim)
    return block


def block_factor(corner, offset, extent, inverse_square, block_edge):
    cells = jnp.arange(extent, dtype=jnp.int32)[:, None]
    shifted = cells - corner[None, :]
    inside = (shifted >= 0) & (shifted < block_edge)
    spread = shifted.astype(jnp.float32) + 0.5 - offset[None, :]
    return jnp.where(inside, jnp.exp(-(spread * spread) * inverse_square[None, :]), 0.0)


def deposit_blocks(arrived, corner_x, corner_z, corner_y, rows_x, rows_z, rows_y, block_edge):
    width = arrived[6]
    inverse_square = 1.0 / (width * width)
    scaled = arrived[0:3] / (math.pi**1.5 * width**3)[None, :]
    along_x = block_factor(corner_x, arrived[3], rows_x, inverse_square, block_edge)
    along_z = block_factor(corner_z, arrived[4], rows_z, inverse_square, block_edge)
    along_y = block_factor(corner_y, arrived[5], rows_y, inverse_square, block_edge)
    left = scaled[:, None, None, :] * along_x[None, :, None, :] * along_z[None, None, :, :]
    left = left.reshape(3 * rows_x * rows_z, -1)
    result = lax.dot_general(
        left,
        along_y,
        (((1,), (1,)), ((), ())),
        precision=lax.Precision.HIGHEST,
        preferred_element_type=jnp.float32,
    )
    return result.reshape(3, rows_x, rows_z, rows_y)


def local(
    velocity,
    point_velocity,
    point_coef,
    point_width,
    send_point,
    send_count,
    slot_offset,
    send_anchor,
    vertical_inverse,
):
    rows_x = velocity.shape[1]
    rows_z = velocity.shape[2]
    rows_y = velocity.shape[3]
    slot_total = send_point.shape[1]
    device_count = lax.axis_size("gx") * lax.axis_size("gy")
    capacity = slot_total // device_count
    records = source_records(
        point_velocity,
        point_coef[None, :],
        point_width[None, :],
        send_point,
        send_count,
        slot_offset[:, 0, :],
    )
    fields = records.shape[1] // capacity
    arrived = lax.all_to_all(records, ("gx", "gy"), split_axis=0, concat_axis=0, tiled=True)
    arrived = arrived.reshape(device_count, fields, capacity).transpose(1, 0, 2)
    arrived = arrived.reshape(fields, slot_total)
    anchors = send_anchor[0]
    corner_x = anchors // (rows_z * rows_y)
    remainder = anchors % (rows_z * rows_y)
    corner_z = remainder // rows_y
    corner_y = remainder % rows_y
    forcing = deposit_blocks(arrived, corner_x, corner_z, corner_y, rows_x, rows_z, rows_y, K)
    wide_x = with_halo(velocity, (("gy", 1),), 1, True)
    wide_z = with_halo(velocity, (("gx", 2),), 1, False)
    grad_x = (wide_x[:, 2:] - wide_x[:, :-2]) * 0.5
    grad_z = (wide_z[:, :, 2:] - wide_z[:, :, :-2]) * 0.5
    grad_y = (jnp.roll(velocity, -1, axis=3) - jnp.roll(velocity, 1, axis=3)) * 0.5
    transport = velocity[0:1] * grad_x + velocity[1:2] * grad_y + velocity[2:3] * grad_z
    updated = velocity + time_step * (forcing - transport)
    columns = lax.all_to_all(updated, "gx", split_axis=1, concat_axis=2, tiled=True)
    solved = jnp.einsum("zk,cxky->cxzy", vertical_inverse, columns, precision=lax.Precision.HIGHEST)
    new_velocity = lax.all_to_all(solved, "gx", split_axis=2, concat_axis=1, tiled=True)
    return new_velocity


def solution(mesh):
    placed = (
        P(None, "gy", "gx", None),
        P(None, ("gx", "gy")),
        P(("gx", "gy")),
        P(("gx", "gy")),
        P(("gx", "gy"), None),
        P(("gx", "gy"), None),
        P(None, ("gx", "gy"), None),
        P(("gx", "gy"), None),
        P(),
    )
    return jax.shard_map(
        local, mesh=mesh, in_specs=placed, out_specs=P(None, "gy", "gx", None), check_vma=False
    )
```

```python
import math

import jax
import jax.numpy as jnp
from jax import lax
from jax.experimental import pallas as pl
from jax.sharding import PartitionSpec as P

HIGHEST = lax.Precision.HIGHEST


def _rows(pieces, shape):
    row = lax.broadcasted_iota(jnp.int32, shape, 0)
    total = jnp.zeros(shape, jnp.float32)
    for k, piece in enumerate(pieces):
        total = jnp.where(row == k, jnp.broadcast_to(piece, shape), total)
    return total


def source_kernel(pv_ref, coef_ref, width_ref, sp_ref, cnt_ref, off_ref, out_ref):
    points = pv_ref.shape[1]
    slots = sp_ref.shape[1]
    tiles = cnt_ref.shape[1]
    capacity = slots // tiles
    fields = out_ref.shape[0]
    pv = pv_ref[...]
    speed = jnp.sqrt(pv[0:1] * pv[0:1] + pv[1:2] * pv[1:2] + pv[2:3] * pv[2:3])
    force = -(coef_ref[...] * speed) * pv
    vals = _rows([force[0:1], force[1:2], force[2:3], width_ref[...]], (8, points))
    pick = (lax.broadcasted_iota(jnp.int32, (points, slots), 0) == sp_ref[...]).astype(jnp.float32)
    picked = jnp.dot(vals, pick, precision=HIGHEST, preferred_element_type=jnp.float32)
    slot_at = lax.broadcasted_iota(jnp.int32, (tiles, slots), 1)
    tile_at = lax.broadcasted_iota(jnp.int32, (tiles, slots), 0)
    tile_of = (slot_at // capacity == tile_at).astype(jnp.float32)
    counts = _rows([cnt_ref[...].astype(jnp.float32)], (8, tiles))
    limit = jnp.dot(counts, tile_of, preferred_element_type=jnp.float32)[0:1]
    lane = (lax.broadcasted_iota(jnp.int32, (1, slots), 1) % capacity).astype(jnp.float32)
    live = jnp.where(lane < limit, 1.0, 0.0)
    out_ref[...] = _rows([picked[0:1] * live, picked[1:2] * live, picked[2:3] * live,
                          off_ref[0, 0:1, :], off_ref[1, 0:1, :], off_ref[2, 0:1, :], picked[3:4]],
                         (fields, slots))


def source_records(pv, coef, width, sp, cnt, off):
    return pl.pallas_call(
        source_kernel,
        out_shape=jax.ShapeDtypeStruct((8, sp.shape[1]), jnp.float32),
    )(pv, coef, width, sp, cnt, off)


K = 4


time_step = 0.25


def with_halo(block, sides, width, periodic):
    for axis, dim in sides:
        count = lax.axis_size(axis)
        forward = [(i, i + 1) for i in range(count - 1)]
        if periodic:
            forward.append((count - 1, 0))
        backward = [(target, source) for source, target in forward]
        low = lax.ppermute(
            lax.slice_in_dim(block, block.shape[dim] - width, None, axis=dim), axis, forward
        )
        high = lax.ppermute(lax.slice_in_dim(block, 0, width, axis=dim), axis, backward)
        block = jnp.concatenate([low, block, high], axis=dim)
    return block


def block_factor(corner, offset, extent, inverse_square, block_edge):
    cells = jnp.arange(extent, dtype=jnp.int32)[:, None]
    shifted = cells - corner[None, :]
    inside = (shifted >= 0) & (shifted < block_edge)
    spread = shifted.astype(jnp.float32) + 0.5 - offset[None, :]
    return jnp.where(inside, jnp.exp(-(spread * spread) * inverse_square[None, :]), 0.0)


def deposit_blocks(arrived, corner_x, corner_z, corner_y, rows_x, rows_z, rows_y, block_edge):
    width = arrived[6]
    inverse_square = 1.0 / (width * width)
    scaled = arrived[0:3] / (math.pi**1.5 * width**3)[None, :]
    along_x = block_factor(corner_x, arrived[3], rows_x, inverse_square, block_edge)
    along_z = block_factor(corner_z, arrived[4], rows_z, inverse_square, block_edge)
    along_y = block_factor(corner_y, arrived[5], rows_y, inverse_square, block_edge)
    left = scaled[:, None, None, :] * along_x[None, :, None, :] * along_z[None, None, :, :]
    left = left.reshape(3 * rows_x * rows_z, -1)
    result = lax.dot_general(
        left,
        along_y,
        (((1,), (1,)), ((), ())),
        precision=lax.Precision.HIGHEST,
        preferred_element_type=jnp.float32,
    )
    return result.reshape(3, rows_x, rows_z, rows_y)


def local(
    velocity,
    point_velocity,
    point_coef,
    point_width,
    send_point,
    send_count,
    slot_offset,
    send_anchor,
    vertical_inverse,
):
    rows_x = velocity.shape[1]
    rows_z = velocity.shape[2]
    rows_y = velocity.shape[3]
    slot_total = send_point.shape[1]
    device_count = lax.axis_size("gx") * lax.axis_size("gy")
    capacity = slot_total // device_count
    records = source_records(
        point_velocity,
        point_coef[None, :],
        point_width[None, :],
        send_point,
        send_count,
        slot_offset,
    )
    fields = records.shape[0]
    records = records.reshape(fields, device_count, capacity).transpose(1, 0, 2)
    records = records.reshape(device_count, fields * capacity)
    arrived = lax.all_to_all(records, ("gx", "gy"), split_axis=0, concat_axis=0, tiled=True)
    arrived = arrived.reshape(device_count, fields, capacity).transpose(1, 0, 2)
    arrived = arrived.reshape(fields, slot_total)
    anchors = send_anchor[0]
    corner_x = anchors // (rows_z * rows_y)
    remainder = anchors % (rows_z * rows_y)
    corner_z = remainder // rows_y
    corner_y = remainder % rows_y
    forcing = deposit_blocks(arrived, corner_x, corner_z, corner_y, rows_x, rows_z, rows_y, K)
    wide_x = with_halo(velocity, (("gy", 1),), 1, True)
    wide_z = with_halo(velocity, (("gx", 2),), 1, False)
    grad_x = (wide_x[:, 2:] - wide_x[:, :-2]) * 0.5
    grad_z = (wide_z[:, :, 2:] - wide_z[:, :, :-2]) * 0.5
    grad_y = (jnp.roll(velocity, -1, axis=3) - jnp.roll(velocity, 1, axis=3)) * 0.5
    transport = velocity[0:1] * grad_x + velocity[1:2] * grad_y + velocity[2:3] * grad_z
    updated = velocity + time_step * (forcing - transport)
    columns = lax.all_to_all(updated, "gx", split_axis=1, concat_axis=2, tiled=True)
    solved = jnp.einsum("zk,cxky->cxzy", vertical_inverse, columns, precision=lax.Precision.HIGHEST)
    new_velocity = lax.all_to_all(solved, "gx", split_axis=2, concat_axis=1, tiled=True)
    return new_velocity


def solution(mesh):
    placed = (
        P(None, "gy", "gx", None),
        P(None, ("gx", "gy")),
        P(("gx", "gy")),
        P(("gx", "gy")),
        P(("gx", "gy"), None),
        P(("gx", "gy"), None),
        P(None, ("gx", "gy"), None),
        P(("gx", "gy"), None),
        P(),
    )
    return jax.shard_map(
        local, mesh=mesh, in_specs=placed, out_specs=P(None, "gy", "gx", None), check_vma=False
    )
```

```python
import math

import jax
import jax.numpy as jnp
from jax import lax
from jax.experimental import pallas as pl
from jax.sharding import PartitionSpec as P


HIGHEST = lax.Precision.HIGHEST


def _rows(pieces, shape):
    row = lax.broadcasted_iota(jnp.int32, shape, 0)
    total = jnp.zeros(shape, jnp.float32)
    for k, piece in enumerate(pieces):
        total = jnp.where(row == k, jnp.broadcast_to(piece, shape), total)
    return total


def source_kernel(pv_ref, coef_ref, width_ref, sp_ref, cnt_ref, off_ref, out_ref):
    points = pv_ref.shape[1]
    slots = sp_ref.shape[1]
    tiles = cnt_ref.shape[1]
    capacity = slots // tiles
    fields = out_ref.shape[0]
    pv = pv_ref[...]
    speed = jnp.sqrt(pv[0:1] * pv[0:1] + pv[1:2] * pv[1:2] + pv[2:3] * pv[2:3])
    force = -(coef_ref[...] * speed) * pv
    vals = _rows([force[0:1], force[1:2], force[2:3], width_ref[...]], (8, points))
    pick = (lax.broadcasted_iota(jnp.int32, (points, slots), 0) == sp_ref[...]).astype(jnp.float32)
    picked = jnp.dot(vals, pick, precision=HIGHEST, preferred_element_type=jnp.float32)
    slot_at = lax.broadcasted_iota(jnp.int32, (tiles, slots), 1)
    tile_at = lax.broadcasted_iota(jnp.int32, (tiles, slots), 0)
    tile_of = (slot_at // capacity == tile_at).astype(jnp.float32)
    counts = _rows([cnt_ref[...].astype(jnp.float32)], (8, tiles))
    limit = jnp.dot(counts, tile_of, preferred_element_type=jnp.float32)[0:1]
    lane = (lax.broadcasted_iota(jnp.int32, (1, slots), 1) % capacity).astype(jnp.float32)
    live = jnp.where(lane < limit, 1.0, 0.0)
    out_ref[...] = _rows([picked[0:1] * live, picked[1:2] * live, picked[2:3] * live,
                          off_ref[0, 0:1, :], off_ref[1, 0:1, :], off_ref[2, 0:1, :], picked[3:4]],
                         (fields, slots))


def source_records(pv, coef, width, sp, cnt, off):
    return pl.pallas_call(
        source_kernel,
        out_shape=jax.ShapeDtypeStruct((8, sp.shape[1]), jnp.float32),
    )(pv, coef, width, sp, cnt, off)


K = 4


time_step = 0.25


def with_halo(block, sides, width, periodic):
    for axis, dim in sides:
        count = lax.axis_size(axis)
        forward = [(i, i + 1) for i in range(count - 1)]
        if periodic:
            forward.append((count - 1, 0))
        backward = [(target, source) for source, target in forward]
        low = lax.ppermute(
            lax.slice_in_dim(block, block.shape[dim] - width, None, axis=dim), axis, forward
        )
        high = lax.ppermute(lax.slice_in_dim(block, 0, width, axis=dim), axis, backward)
        block = jnp.concatenate([low, block, high], axis=dim)
    return block


def block_factor(corner, offset, extent, inverse_square, block_edge):
    cells = jnp.arange(extent, dtype=jnp.int32)[:, None]
    shifted = cells - corner[None, :]
    inside = (shifted >= 0) & (shifted < block_edge)
    spread = shifted.astype(jnp.float32) + 0.5 - offset[None, :]
    return jnp.where(inside, jnp.exp(-(spread * spread) * inverse_square[None, :]), 0.0)


def deposit_blocks(arrived, corner_x, corner_z, corner_y, rows_x, rows_z, rows_y, block_edge):
    width = arrived[6]
    inverse_square = 1.0 / (width * width)
    scaled = arrived[0:3] / (math.pi**1.5 * width**3)[None, :]
    along_x = block_factor(corner_x, arrived[3], rows_x, inverse_square, block_edge)
    along_z = block_factor(corner_z, arrived[4], rows_z, inverse_square, block_edge)
    along_y = block_factor(corner_y, arrived[5], rows_y, inverse_square, block_edge)
    left = scaled[:, None, None, :] * along_x[None, :, None, :] * along_z[None, None, :, :]
    left = left.reshape(3 * rows_x * rows_z, -1)
    result = lax.dot_general(
        left,
        along_y,
        (((1,), (1,)), ((), ())),
        precision=lax.Precision.HIGH,
        preferred_element_type=jnp.float32,
    )
    return result.reshape(3, rows_x, rows_z, rows_y)


def local(
    velocity,
    point_velocity,
    point_coef,
    point_width,
    send_point,
    send_count,
    slot_offset,
    send_anchor,
    vertical_inverse,
):
    rows_x = velocity.shape[1]
    rows_z = velocity.shape[2]
    rows_y = velocity.shape[3]
    slot_total = send_point.shape[1]
    device_count = lax.axis_size("gx") * lax.axis_size("gy")
    capacity = slot_total // device_count
    records = source_records(
        point_velocity,
        point_coef[None, :],
        point_width[None, :],
        send_point,
        send_count,
        slot_offset,
    )
    fields = records.shape[0]
    records = records.reshape(fields, device_count, capacity).transpose(1, 0, 2)
    records = records.reshape(device_count, fields * capacity)
    arrived = lax.all_to_all(records, ("gx", "gy"), split_axis=0, concat_axis=0, tiled=True)
    arrived = arrived.reshape(device_count, fields, capacity).transpose(1, 0, 2)
    arrived = arrived.reshape(fields, slot_total)
    anchors = send_anchor[0]
    corner_x = anchors // (rows_z * rows_y)
    remainder = anchors % (rows_z * rows_y)
    corner_z = remainder // rows_y
    corner_y = remainder % rows_y
    forcing = deposit_blocks(arrived, corner_x, corner_z, corner_y, rows_x, rows_z, rows_y, K)
    wide_x = with_halo(velocity, (("gy", 1),), 1, True)
    grad_x = (wide_x[:, 2:] - wide_x[:, :-2]) * 0.5
    grad_y = (jnp.roll(velocity, -1, axis=3) - jnp.roll(velocity, 1, axis=3)) * 0.5
    flat_part = velocity[0:1] * grad_x + velocity[1:2] * grad_y
    partial = velocity + time_step * (forcing - flat_part)
    both = jnp.concatenate([velocity, partial], axis=0)
    columns = lax.all_to_all(both, "gx", split_axis=1, concat_axis=2, tiled=True)
    column_velocity = columns[0:3]
    padded = jnp.pad(column_velocity, ((0, 0), (0, 0), (1, 1), (0, 0)))
    grad_z = (padded[:, :, 2:] - padded[:, :, :-2]) * 0.5
    columns = columns[3:6] - time_step * (column_velocity[2:3] * grad_z)
    solved = jnp.einsum("zk,cxky->cxzy", vertical_inverse, columns, precision=lax.Precision.HIGHEST)
    new_velocity = lax.all_to_all(solved, "gx", split_axis=2, concat_axis=1, tiled=True)
    return new_velocity


def solution(mesh):
    placed = (
        P(None, "gy", "gx", None),
        P(None, ("gx", "gy")),
        P(("gx", "gy")),
        P(("gx", "gy")),
        P(("gx", "gy"), None),
        P(("gx", "gy"), None),
        P(None, ("gx", "gy"), None),
        P(("gx", "gy"), None),
        P(),
    )

    return jax.shard_map(
        local, mesh=mesh, in_specs=placed, out_specs=P(None, "gy", "gx", None), check_vma=False
    )
```

```python
import functools
import math

import jax
import jax.numpy as jnp
from jax import lax
from jax.experimental import pallas as pl
from jax.sharding import PartitionSpec as P


def _rows(pieces, shape):
    row = lax.broadcasted_iota(jnp.int32, shape, 0)
    total = jnp.zeros(shape, jnp.float32)
    for k, piece in enumerate(pieces):
        total = jnp.where(row == k, jnp.broadcast_to(piece, shape), total)
    return total


def _pieces(x):
    high = x.astype(jnp.bfloat16)
    rest = x - high.astype(jnp.float32)
    middle = rest.astype(jnp.bfloat16)
    low = (rest - middle.astype(jnp.float32)).astype(jnp.bfloat16)
    return high, middle, low


def _exact_dot(values, pick, dims):
    total = None
    for piece in _pieces(values):
        term = lax.dot_general(piece, pick, dims, preferred_element_type=jnp.float32)
        total = term if total is None else total + term
    return total


def _exact_dot_picked_right(pick, values, dims):
    total = None
    for piece in _pieces(values):
        term = lax.dot_general(pick, piece, dims, preferred_element_type=jnp.float32)
        total = term if total is None else total + term
    return total


def source_kernel(pv_ref, coef_ref, width_ref, sp_ref, cnt_ref, off_ref, out_ref):
    points = pv_ref.shape[1]
    slots = sp_ref.shape[1]
    tiles = cnt_ref.shape[1]
    capacity = slots // tiles
    lanes_out = out_ref.shape[1]
    fields = lanes_out // capacity
    plain = (((1,), (0,)), ((), ()))
    pv = pv_ref[...]
    speed = jnp.sqrt(pv[0:1] * pv[0:1] + pv[1:2] * pv[1:2] + pv[2:3] * pv[2:3])
    force = -(coef_ref[...] * speed) * pv
    vals = _rows([force[0:1], force[1:2], force[2:3], width_ref[...]], (8, points))
    pick = (lax.broadcasted_iota(jnp.int32, (points, slots), 0) == sp_ref[...]).astype(jnp.bfloat16)
    picked = _exact_dot(vals, pick, plain)
    slot_at = lax.broadcasted_iota(jnp.int32, (tiles, slots), 1)
    tile_at = lax.broadcasted_iota(jnp.int32, (tiles, slots), 0)
    tile_of = (slot_at // capacity == tile_at).astype(jnp.bfloat16)
    counts = _rows([cnt_ref[...].astype(jnp.float32)], (8, tiles)).astype(jnp.bfloat16)
    limit = lax.dot_general(counts, tile_of, plain, preferred_element_type=jnp.float32)[0:1]
    lane = (lax.broadcasted_iota(jnp.int32, (1, slots), 1) % capacity).astype(jnp.float32)
    live = jnp.where(lane < limit, 1.0, 0.0)
    table = _rows([picked[0:1] * live, picked[1:2] * live, picked[2:3] * live,
                   off_ref[0, 0:1, :], off_ref[1, 0:1, :], off_ref[2, 0:1, :], picked[3:4]],
                  (fields, slots))
    spread = jnp.concatenate(
        [jnp.broadcast_to(table[v:v + 1], (capacity, slots)) for v in range(fields)], axis=0)
    same_c = (lax.broadcasted_iota(jnp.int32, (lanes_out, slots), 1) % capacity
              == lax.broadcasted_iota(jnp.int32, (lanes_out, slots), 0) % capacity)
    spread = jnp.where(same_c, spread, 0.0)
    out_ref[...] = _exact_dot_picked_right(tile_of, spread, (((1,), (1,)), ((), ())))


def source_records(pv, coef, width, sp, cnt, off):
    tiles = cnt.shape[1]
    capacity = sp.shape[1] // tiles
    return pl.pallas_call(
        source_kernel,
        out_shape=jax.ShapeDtypeStruct((tiles, 8 * capacity), jnp.float32),
    )(pv, coef, width, sp, cnt, off)


K = 4


time_step = 0.25


def with_halo(block, sides, width, periodic):
    for axis, dim in sides:
        count = lax.axis_size(axis)
        forward = [(i, i + 1) for i in range(count - 1)]
        if periodic:
            forward.append((count - 1, 0))
        backward = [(target, source) for source, target in forward]
        low = lax.ppermute(
            lax.slice_in_dim(block, block.shape[dim] - width, None, axis=dim), axis, forward
        )
        high = lax.ppermute(lax.slice_in_dim(block, 0, width, axis=dim), axis, backward)
        block = jnp.concatenate([low, block, high], axis=dim)
    return block


def deposit_kernel(arrived_ref, anchor_ref, out_ref, *, rows_x, rows_z, rows_y, block_edge):
    sources, _ = arrived_ref.shape
    capacity = anchor_ref.shape[1]
    cells = rows_x * rows_z
    width_out = 3 * cells
    lane = lax.broadcasted_iota(jnp.int32, (sources, width_out), 1)
    comp = lane // cells
    cell_x = (lane // rows_z) % rows_x
    cell_z = lane % rows_z
    cell_y = lax.broadcasted_iota(jnp.int32, (sources, rows_y), 1)
    norm = 1.0 / math.pi**1.5

    def group(c, total):
        rec = arrived_ref[...]
        pick = lambda v: rec[:, v * capacity + c : v * capacity + c + 1]
        anchor = anchor_ref[:, c : c + 1]
        corner_x = anchor // (rows_z * rows_y)
        corner_z = (anchor // rows_y) % rows_z
        corner_y = anchor % rows_y
        width = pick(6)
        inverse_square = 1.0 / (width * width)
        scale = norm / (width * width * width)
        dx = cell_x - corner_x
        dz = cell_z - corner_z
        inside = (dx >= 0) & (dx < block_edge) & (dz >= 0) & (dz < block_edge)
        rx = dx.astype(jnp.float32) + 0.5 - pick(3)
        rz = dz.astype(jnp.float32) + 0.5 - pick(4)
        force = jnp.where(comp == 0, pick(0), jnp.where(comp == 1, pick(1), pick(2)))
        left = jnp.where(inside, force * scale * jnp.exp(-(rx * rx + rz * rz) * inverse_square), 0.0)
        dy = cell_y - corner_y
        ry = dy.astype(jnp.float32) + 0.5 - pick(5)
        along_y = jnp.where((dy >= 0) & (dy < block_edge), jnp.exp(-(ry * ry) * inverse_square), 0.0)
        return total + lax.dot_general(left, along_y, (((0,), (0,)), ((), ())),
                                       precision=lax.Precision.HIGHEST,
                                       preferred_element_type=jnp.float32)

    total = jnp.zeros(out_ref.shape, jnp.float32)
    for c in range(capacity):
        total = group(c, total)
    out_ref[...] = total


def deposit_records(arrived, anchors, rows_x, rows_z, rows_y, block_edge):
    kernel = functools.partial(deposit_kernel, rows_x=rows_x, rows_z=rows_z, rows_y=rows_y,
                               block_edge=block_edge)
    return pl.pallas_call(
        kernel,
        out_shape=jax.ShapeDtypeStruct((3 * rows_x * rows_z, rows_y), jnp.float32),
    )(arrived, anchors)


def local(
    velocity,
    point_velocity,
    point_coef,
    point_width,
    send_point,
    send_count,
    slot_offset,
    send_anchor,
    vertical_inverse,
):
    rows_x = velocity.shape[1]
    rows_z = velocity.shape[2]
    rows_y = velocity.shape[3]
    slot_total = send_point.shape[1]
    device_count = lax.axis_size("gx") * lax.axis_size("gy")
    capacity = slot_total // device_count
    records = source_records(
        point_velocity,
        point_coef[None, :],
        point_width[None, :],
        send_point,
        send_count,
        slot_offset,
    )
    arrived = lax.all_to_all(records, ("gx", "gy"), split_axis=0, concat_axis=0, tiled=True)
    anchors = send_anchor.reshape(device_count, capacity)
    forcing = deposit_records(arrived, anchors, rows_x, rows_z, rows_y, K)
    forcing = forcing.reshape(3, rows_x, rows_z, rows_y)
    wide_x = with_halo(velocity, (("gy", 1),), 1, True)
    grad_x = (wide_x[:, 2:] - wide_x[:, :-2]) * 0.5
    grad_y = (jnp.roll(velocity, -1, axis=3) - jnp.roll(velocity, 1, axis=3)) * 0.5
    flat_part = velocity[0:1] * grad_x + velocity[1:2] * grad_y
    partial = velocity + time_step * (forcing - flat_part)
    both = jnp.concatenate([velocity, partial], axis=0)
    columns = lax.all_to_all(both, "gx", split_axis=1, concat_axis=2, tiled=True)
    column_velocity = columns[0:3]
    padded = jnp.pad(column_velocity, ((0, 0), (0, 0), (1, 1), (0, 0)))
    grad_z = (padded[:, :, 2:] - padded[:, :, :-2]) * 0.5
    columns = columns[3:6] - time_step * (column_velocity[2:3] * grad_z)
    solved = jnp.einsum("zk,cxky->cxzy", vertical_inverse, columns, precision=lax.Precision.HIGHEST)
    new_velocity = lax.all_to_all(solved, "gx", split_axis=2, concat_axis=1, tiled=True)
    return new_velocity


def solution(mesh):
    placed = (
        P(None, "gy", "gx", None),
        P(None, ("gx", "gy")),
        P(("gx", "gy")),
        P(("gx", "gy")),
        P(("gx", "gy"), None),
        P(("gx", "gy"), None),
        P(None, ("gx", "gy"), None),
        P(("gx", "gy"), None),
        P(),
    )

    return jax.shard_map(
        local, mesh=mesh, in_specs=placed, out_specs=P(None, "gy", "gx", None), check_vma=False
    )
```

```python
import math

import jax
import jax.numpy as jnp
from jax import lax
from jax.experimental import pallas as pl
from jax.sharding import PartitionSpec as P


def _rows(pieces, shape):
    row = lax.broadcasted_iota(jnp.int32, shape, 0)
    total = jnp.zeros(shape, jnp.float32)
    for k, piece in enumerate(pieces):
        total = jnp.where(row == k, jnp.broadcast_to(piece, shape), total)
    return total


def _pieces(x):
    high = x.astype(jnp.bfloat16)
    rest = x - high.astype(jnp.float32)
    middle = rest.astype(jnp.bfloat16)
    low = (rest - middle.astype(jnp.float32)).astype(jnp.bfloat16)
    return high, middle, low


def _exact_dot(values, pick, dims):
    total = None
    for piece in _pieces(values):
        term = lax.dot_general(piece, pick, dims, preferred_element_type=jnp.float32)
        total = term if total is None else total + term
    return total


def _exact_dot_picked_right(pick, values, dims):
    total = None
    for piece in _pieces(values):
        term = lax.dot_general(pick, piece, dims, preferred_element_type=jnp.float32)
        total = term if total is None else total + term
    return total


def source_kernel(pv_ref, coef_ref, width_ref, sp_ref, cnt_ref, off_ref, out_ref):
    points = pv_ref.shape[1]
    slots = sp_ref.shape[1]
    tiles = cnt_ref.shape[1]
    capacity = slots // tiles
    lanes_out = out_ref.shape[1]
    fields = lanes_out // capacity
    plain = (((1,), (0,)), ((), ()))
    pv = pv_ref[...]
    speed = jnp.sqrt(pv[0:1] * pv[0:1] + pv[1:2] * pv[1:2] + pv[2:3] * pv[2:3])
    force = -(coef_ref[...] * speed) * pv
    vals = _rows([force[0:1], force[1:2], force[2:3], width_ref[...]], (8, points))
    pick = (lax.broadcasted_iota(jnp.int32, (points, slots), 0) == sp_ref[...]).astype(jnp.bfloat16)
    picked = _exact_dot(vals, pick, plain)
    slot_at = lax.broadcasted_iota(jnp.int32, (tiles, slots), 1)
    tile_at = lax.broadcasted_iota(jnp.int32, (tiles, slots), 0)
    tile_of = (slot_at // capacity == tile_at).astype(jnp.bfloat16)
    counts = _rows([cnt_ref[...].astype(jnp.float32)], (8, tiles)).astype(jnp.bfloat16)
    limit = lax.dot_general(counts, tile_of, plain, preferred_element_type=jnp.float32)[0:1]
    lane = (lax.broadcasted_iota(jnp.int32, (1, slots), 1) % capacity).astype(jnp.float32)
    live = jnp.where(lane < limit, 1.0, 0.0)
    table = _rows([picked[0:1] * live, picked[1:2] * live, picked[2:3] * live,
                   off_ref[0, 0:1, :], off_ref[1, 0:1, :], off_ref[2, 0:1, :], picked[3:4]],
                  (fields, slots))
    spread = jnp.concatenate(
        [jnp.broadcast_to(table[v:v + 1], (capacity, slots)) for v in range(fields)], axis=0)
    same_c = (lax.broadcasted_iota(jnp.int32, (lanes_out, slots), 1) % capacity
              == lax.broadcasted_iota(jnp.int32, (lanes_out, slots), 0) % capacity)
    spread = jnp.where(same_c, spread, 0.0)
    out_ref[...] = _exact_dot_picked_right(tile_of, spread, (((1,), (1,)), ((), ())))


def source_records(pv, coef, width, sp, cnt, off):
    tiles = cnt.shape[1]
    capacity = sp.shape[1] // tiles
    return pl.pallas_call(
        source_kernel,
        out_shape=jax.ShapeDtypeStruct((tiles, 8 * capacity), jnp.float32),
    )(pv, coef, width, sp, cnt, off)


K = 4


time_step = 0.25


def with_halo(block, sides, width, periodic):
    for axis, dim in sides:
        count = lax.axis_size(axis)
        forward = [(i, i + 1) for i in range(count - 1)]
        if periodic:
            forward.append((count - 1, 0))
        backward = [(target, source) for source, target in forward]
        low = lax.ppermute(
            lax.slice_in_dim(block, block.shape[dim] - width, None, axis=dim), axis, forward
        )
        high = lax.ppermute(lax.slice_in_dim(block, 0, width, axis=dim), axis, backward)
        block = jnp.concatenate([low, block, high], axis=dim)
    return block


def block_factor(corner, offset, extent, inverse_square, block_edge):
    cells = jnp.arange(extent, dtype=jnp.int32)[:, None]
    shifted = cells - corner[None, :]
    inside = (shifted >= 0) & (shifted < block_edge)
    spread = shifted.astype(jnp.float32) + 0.5 - offset[None, :]
    return jnp.where(inside, jnp.exp(-(spread * spread) * inverse_square[None, :]), 0.0)


def deposit_blocks(arrived, corner_x, corner_z, corner_y, rows_x, rows_z, rows_y, block_edge):
    width = arrived[6]
    inverse_square = 1.0 / (width * width)
    scaled = arrived[0:3] / (math.pi**1.5 * width**3)[None, :]
    along_x = block_factor(corner_x, arrived[3], rows_x, inverse_square, block_edge)
    along_z = block_factor(corner_z, arrived[4], rows_z, inverse_square, block_edge)
    along_y = block_factor(corner_y, arrived[5], rows_y, inverse_square, block_edge)
    left = scaled[:, None, None, :] * along_x[None, :, None, :] * along_z[None, None, :, :]
    left = left.reshape(3 * rows_x * rows_z, -1)
    result = lax.dot_general(
        left,
        along_y,
        (((1,), (1,)), ((), ())),
        precision=lax.Precision.HIGH,
        preferred_element_type=jnp.float32,
    )
    return result.reshape(3, rows_x, rows_z, rows_y)


def local(
    velocity,
    point_velocity,
    point_coef,
    point_width,
    send_point,
    send_count,
    slot_offset,
    send_anchor,
    vertical_inverse,
):
    rows_x = velocity.shape[1]
    rows_z = velocity.shape[2]
    rows_y = velocity.shape[3]
    slot_total = send_point.shape[1]
    device_count = lax.axis_size("gx") * lax.axis_size("gy")
    capacity = slot_total // device_count
    records = source_records(
        point_velocity,
        point_coef[None, :],
        point_width[None, :],
        send_point,
        send_count,
        slot_offset,
    )
    fields = records.shape[1] // capacity
    arrived = lax.all_to_all(records, ("gx", "gy"), split_axis=0, concat_axis=0, tiled=True)
    arrived = arrived.reshape(device_count, fields, capacity).transpose(1, 0, 2)
    arrived = arrived.reshape(fields, slot_total)
    anchors = send_anchor[0]
    corner_x = anchors // (rows_z * rows_y)
    remainder = anchors % (rows_z * rows_y)
    corner_z = remainder // rows_y
    corner_y = remainder % rows_y
    forcing = deposit_blocks(arrived, corner_x, corner_z, corner_y, rows_x, rows_z, rows_y, K)
    wide_x = with_halo(velocity, (("gy", 1),), 1, True)
    grad_x = (wide_x[:, 2:] - wide_x[:, :-2]) * 0.5
    grad_y = (jnp.roll(velocity, -1, axis=3) - jnp.roll(velocity, 1, axis=3)) * 0.5
    flat_part = velocity[0:1] * grad_x + velocity[1:2] * grad_y
    partial = velocity + time_step * (forcing - flat_part)
    both = jnp.concatenate([velocity, partial], axis=0)
    columns = lax.all_to_all(both, "gx", split_axis=1, concat_axis=2, tiled=True)
    column_velocity = columns[0:3]
    padded = jnp.pad(column_velocity, ((0, 0), (0, 0), (1, 1), (0, 0)))
    grad_z = (padded[:, :, 2:] - padded[:, :, :-2]) * 0.5
    columns = columns[3:6] - time_step * (column_velocity[2:3] * grad_z)
    solved = jnp.einsum("zk,cxky->cxzy", vertical_inverse, columns, precision=lax.Precision.HIGHEST)
    solved = solved.reshape(3, rows_x, rows_z, rows_y)
    new_velocity = lax.all_to_all(solved, "gx", split_axis=1, concat_axis=1, tiled=True)
    return new_velocity


def solution(mesh):
    placed = (
        P(None, "gy", "gx", None),
        P(None, ("gx", "gy")),
        P(("gx", "gy")),
        P(("gx", "gy")),
        P(("gx", "gy"), None),
        P(("gx", "gy"), None),
        P(None, ("gx", "gy"), None),
        P(("gx", "gy"), None),
        P(),
    )

    return jax.shard_map(
        local, mesh=mesh, in_specs=placed, out_specs=P(None, "gy", "gx", None), check_vma=False
    )
```

```python
import math

import jax
import jax.numpy as jnp
from jax import lax
from jax.experimental import pallas as pl
from jax.sharding import PartitionSpec as P


def _rows(pieces, shape):
    row = lax.broadcasted_iota(jnp.int32, shape, 0)
    total = jnp.zeros(shape, jnp.float32)
    for k, piece in enumerate(pieces):
        total = jnp.where(row == k, jnp.broadcast_to(piece, shape), total)
    return total


def _pieces(x):
    high = x.astype(jnp.bfloat16)
    rest = x - high.astype(jnp.float32)
    middle = rest.astype(jnp.bfloat16)
    low = (rest - middle.astype(jnp.float32)).astype(jnp.bfloat16)
    return high, middle, low


def _exact_dot(values, pick, dims):
    total = None
    for piece in _pieces(values):
        term = lax.dot_general(piece, pick, dims, preferred_element_type=jnp.float32)
        total = term if total is None else total + term
    return total


def source_kernel(pv_ref, coef_ref, width_ref, sp_ref, cnt_ref, off_ref, out_ref):
    points = pv_ref.shape[1]
    slots = sp_ref.shape[1]
    tiles = cnt_ref.shape[1]
    capacity = slots // tiles
    lanes_out = out_ref.shape[1]
    fields = lanes_out // capacity
    plain = (((1,), (0,)), ((), ()))
    pv = pv_ref[...]
    speed = jnp.sqrt(pv[0:1] * pv[0:1] + pv[1:2] * pv[1:2] + pv[2:3] * pv[2:3])
    force = -(coef_ref[...] * speed) * pv
    vals = _rows([force[0:1], force[1:2], force[2:3], width_ref[...]], (8, points))
    pick = (lax.broadcasted_iota(jnp.int32, (points, slots), 0) == sp_ref[...]).astype(jnp.bfloat16)
    picked = _exact_dot(vals, pick, plain)
    slot_at = lax.broadcasted_iota(jnp.int32, (tiles, slots), 1)
    tile_at = lax.broadcasted_iota(jnp.int32, (tiles, slots), 0)
    tile_of = (slot_at // capacity == tile_at).astype(jnp.bfloat16)
    counts = _rows([cnt_ref[...].astype(jnp.float32)], (8, tiles)).astype(jnp.bfloat16)
    limit = lax.dot_general(counts, tile_of, plain, preferred_element_type=jnp.float32)[0:1]
    lane = (lax.broadcasted_iota(jnp.int32, (1, slots), 1) % capacity).astype(jnp.float32)
    live = jnp.where(lane < limit, 1.0, 0.0)
    table = _rows([picked[0:1] * live, picked[1:2] * live, picked[2:3] * live,
                   off_ref[0, 0:1, :], off_ref[1, 0:1, :], off_ref[2, 0:1, :], picked[3:4]],
                  (fields, slots))
    spread = jnp.concatenate(
        [jnp.broadcast_to(table[v:v + 1], (capacity, slots)) for v in range(fields)], axis=0)
    same_c = (lax.broadcasted_iota(jnp.int32, (lanes_out, slots), 1) % capacity
              == lax.broadcasted_iota(jnp.int32, (lanes_out, slots), 0) % capacity)
    spread = jnp.where(same_c, spread, 0.0)
    slot_row = lax.broadcasted_iota(jnp.int32, (slots, tiles), 0)
    tile_col = lax.broadcasted_iota(jnp.int32, (slots, tiles), 1)
    slot_tile = (slot_row // capacity == tile_col).astype(jnp.bfloat16)
    out_ref[...] = _exact_dot(spread, slot_tile, plain).T


def source_records(pv, coef, width, sp, cnt, off):
    tiles = cnt.shape[1]
    capacity = sp.shape[1] // tiles
    return pl.pallas_call(
        source_kernel,
        out_shape=jax.ShapeDtypeStruct((tiles, 8 * capacity), jnp.float32),
    )(pv, coef, width, sp, cnt, off)


K = 4


time_step = 0.25


def with_halo(block, sides, width, periodic):
    for axis, dim in sides:
        count = lax.axis_size(axis)
        forward = [(i, i + 1) for i in range(count - 1)]
        if periodic:
            forward.append((count - 1, 0))
        backward = [(target, source) for source, target in forward]
        low = lax.ppermute(
            lax.slice_in_dim(block, block.shape[dim] - width, None, axis=dim), axis, forward
        )
        high = lax.ppermute(lax.slice_in_dim(block, 0, width, axis=dim), axis, backward)
        block = jnp.concatenate([low, block, high], axis=dim)
    return block


def block_factor(corner, offset, extent, inverse_square, block_edge):
    cells = jnp.arange(extent, dtype=jnp.int32)[:, None]
    shifted = cells - corner[None, :]
    inside = (shifted >= 0) & (shifted < block_edge)
    spread = shifted.astype(jnp.float32) + 0.5 - offset[None, :]
    return jnp.where(inside, jnp.exp(-(spread * spread) * inverse_square[None, :]), 0.0)


def deposit_blocks(arrived, corner_x, corner_z, corner_y, rows_x, rows_z, rows_y, block_edge):
    width = arrived[6]
    inverse_square = 1.0 / (width * width)
    scaled = arrived[0:3] / (math.pi**1.5 * width**3)[None, :]
    along_x = block_factor(corner_x, arrived[3], rows_x, inverse_square, block_edge)
    along_z = block_factor(corner_z, arrived[4], rows_z, inverse_square, block_edge)
    along_y = block_factor(corner_y, arrived[5], rows_y, inverse_square, block_edge)
    left = scaled[:, None, None, :] * along_x[None, :, None, :] * along_z[None, None, :, :]
    left = left.reshape(3 * rows_x * rows_z, -1)
    result = lax.dot_general(
        left,
        along_y,
        (((1,), (1,)), ((), ())),
        precision=lax.Precision.HIGH,
        preferred_element_type=jnp.float32,
    )
    return result.reshape(3, rows_x, rows_z, rows_y)


def local(
    velocity,
    point_velocity,
    point_coef,
    point_width,
    send_point,
    send_count,
    slot_offset,
    send_anchor,
    vertical_inverse,
):
    rows_x = velocity.shape[1]
    rows_z = velocity.shape[2]
    rows_y = velocity.shape[3]
    slot_total = send_point.shape[1]
    device_count = lax.axis_size("gx") * lax.axis_size("gy")
    capacity = slot_total // device_count
    records = source_records(
        point_velocity,
        point_coef[None, :],
        point_width[None, :],
        send_point,
        send_count,
        slot_offset,
    )
    fields = records.shape[1] // capacity
    arrived = lax.all_to_all(records, ("gx", "gy"), split_axis=0, concat_axis=0, tiled=True)
    arrived = arrived.reshape(device_count, fields, capacity).transpose(1, 0, 2)
    arrived = arrived.reshape(fields, slot_total)
    anchors = send_anchor[0]
    corner_x = anchors // (rows_z * rows_y)
    remainder = anchors % (rows_z * rows_y)
    corner_z = remainder // rows_y
    corner_y = remainder % rows_y
    forcing = deposit_blocks(arrived, corner_x, corner_z, corner_y, rows_x, rows_z, rows_y, K)
    wide_x = with_halo(velocity, (("gy", 1),), 1, True)
    grad_x = (wide_x[:, 2:] - wide_x[:, :-2]) * 0.5
    grad_y = (jnp.roll(velocity, -1, axis=3) - jnp.roll(velocity, 1, axis=3)) * 0.5
    flat_part = velocity[0:1] * grad_x + velocity[1:2] * grad_y
    partial = velocity + time_step * (forcing - flat_part)
    both = jnp.concatenate([velocity, partial], axis=0)
    columns = lax.all_to_all(both, "gx", split_axis=1, concat_axis=2, tiled=True)
    column_velocity = columns[0:3]
    padded = jnp.pad(column_velocity, ((0, 0), (0, 0), (1, 1), (0, 0)))
    grad_z = (padded[:, :, 2:] - padded[:, :, :-2]) * 0.5
    columns = columns[3:6] - time_step * (column_velocity[2:3] * grad_z)
    solved = jnp.einsum("zk,cxky->cxzy", vertical_inverse, columns, precision=lax.Precision.HIGHEST)
    solved = solved.reshape(3, rows_x, rows_z, rows_y)
    new_velocity = lax.all_to_all(solved, "gx", split_axis=1, concat_axis=1, tiled=True)
    return new_velocity


def solution(mesh):
    placed = (
        P(None, "gy", "gx", None),
        P(None, ("gx", "gy")),
        P(("gx", "gy")),
        P(("gx", "gy")),
        P(("gx", "gy"), None),
        P(("gx", "gy"), None),
        P(None, ("gx", "gy"), None),
        P(("gx", "gy"), None),
        P(),
    )

    return jax.shard_map(
        local, mesh=mesh, in_specs=placed, out_specs=P(None, "gy", "gx", None), check_vma=False
    )
```

```python
import math

import jax
import jax.numpy as jnp
from jax import lax
from jax.experimental import pallas as pl
from jax.sharding import PartitionSpec as P


def _rows(pieces, shape):
    row = lax.broadcasted_iota(jnp.int32, shape, 0)
    total = jnp.zeros(shape, jnp.float32)
    for k, piece in enumerate(pieces):
        total = jnp.where(row == k, jnp.broadcast_to(piece, shape), total)
    return total


def _pieces(x):
    high = x.astype(jnp.bfloat16)
    rest = x - high.astype(jnp.float32)
    middle = rest.astype(jnp.bfloat16)
    low = (rest - middle.astype(jnp.float32)).astype(jnp.bfloat16)
    return high, middle, low


def _exact_dot(values, pick, dims):
    total = None
    for piece in _pieces(values):
        term = lax.dot_general(piece, pick, dims, preferred_element_type=jnp.float32)
        total = term if total is None else total + term
    return total


def source_kernel(pv_ref, coef_ref, width_ref, sp_ref, cnt_ref, off_ref, out_ref):
    points = pv_ref.shape[1]
    slots = sp_ref.shape[1]
    tiles = cnt_ref.shape[1]
    capacity = slots // tiles
    lanes_out = out_ref.shape[1]
    fields = lanes_out // capacity
    plain = (((1,), (0,)), ((), ()))
    pv = pv_ref[...]
    speed = jnp.sqrt(pv[0:1] * pv[0:1] + pv[1:2] * pv[1:2] + pv[2:3] * pv[2:3])
    force = -(coef_ref[...] * speed) * pv
    vals = _rows([force[0:1], force[1:2], force[2:3], width_ref[...]], (8, points))
    pick = (lax.broadcasted_iota(jnp.int32, (points, slots), 0) == sp_ref[...]).astype(jnp.bfloat16)
    picked = _exact_dot(vals, pick, plain)
    slot_at = lax.broadcasted_iota(jnp.int32, (tiles, slots), 1)
    tile_at = lax.broadcasted_iota(jnp.int32, (tiles, slots), 0)
    tile_of = (slot_at // capacity == tile_at).astype(jnp.bfloat16)
    counts = _rows([cnt_ref[...].astype(jnp.float32)], (8, tiles)).astype(jnp.bfloat16)
    limit = lax.dot_general(counts, tile_of, plain, preferred_element_type=jnp.float32)[0:1]
    lane = (lax.broadcasted_iota(jnp.int32, (1, slots), 1) % capacity).astype(jnp.float32)
    live = jnp.where(lane < limit, 1.0, 0.0)
    table = _rows([picked[0:1] * live, picked[1:2] * live, picked[2:3] * live,
                   off_ref[0, 0:1, :], off_ref[1, 0:1, :], off_ref[2, 0:1, :], picked[3:4]],
                  (fields, slots))
    spread = jnp.concatenate(
        [jnp.broadcast_to(table[v:v + 1], (capacity, slots)) for v in range(fields)], axis=0)
    same_c = (lax.broadcasted_iota(jnp.int32, (lanes_out, slots), 1) % capacity
              == lax.broadcasted_iota(jnp.int32, (lanes_out, slots), 0) % capacity)
    spread = jnp.where(same_c, spread, 0.0)
    slot_row = lax.broadcasted_iota(jnp.int32, (slots, tiles), 0)
    tile_col = lax.broadcasted_iota(jnp.int32, (slots, tiles), 1)
    slot_tile = (slot_row // capacity == tile_col).astype(jnp.bfloat16)
    out_ref[...] = _exact_dot(spread, slot_tile, plain).T


def source_records(pv, coef, width, sp, cnt, off):
    tiles = cnt.shape[1]
    capacity = sp.shape[1] // tiles
    return pl.pallas_call(
        source_kernel,
        out_shape=jax.ShapeDtypeStruct((tiles, 8 * capacity), jnp.float32),
    )(pv, coef, width, sp, cnt, off)


K = 4


time_step = 0.25


def with_halo(block, sides, width, periodic):
    for axis, dim in sides:
        count = lax.axis_size(axis)
        forward = [(i, i + 1) for i in range(count - 1)]
        if periodic:
            forward.append((count - 1, 0))
        backward = [(target, source) for source, target in forward]
        low = lax.ppermute(
            lax.slice_in_dim(block, block.shape[dim] - width, None, axis=dim), axis, forward
        )
        high = lax.ppermute(lax.slice_in_dim(block, 0, width, axis=dim), axis, backward)
        block = jnp.concatenate([low, block, high], axis=dim)
    return block


def block_factor(corner, offset, extent, inverse_square, block_edge):
    cells = jnp.arange(extent, dtype=jnp.int32)[:, None]
    shifted = cells - corner[None, :]
    inside = (shifted >= 0) & (shifted < block_edge)
    spread = shifted.astype(jnp.float32) + 0.5 - offset[None, :]
    return jnp.where(inside, jnp.exp(-(spread * spread) * inverse_square[None, :]), 0.0)


def deposit_blocks(arrived, corner_x, corner_z, corner_y, rows_x, rows_z, rows_y, block_edge):
    width = arrived[6]
    inverse_square = 1.0 / (width * width)
    scaled = arrived[0:3] / (math.pi**1.5 * width**3)[None, :]
    along_x = block_factor(corner_x, arrived[3], rows_x, inverse_square, block_edge)
    along_z = block_factor(corner_z, arrived[4], rows_z, inverse_square, block_edge)
    along_y = block_factor(corner_y, arrived[5], rows_y, inverse_square, block_edge)
    left = scaled[:, None, None, :] * along_x[None, :, None, :] * along_z[None, None, :, :]
    left = left.reshape(3 * rows_x * rows_z, -1)
    result = lax.dot_general(
        left,
        along_y,
        (((1,), (1,)), ((), ())),
        precision=lax.Precision.HIGH,
        preferred_element_type=jnp.float32,
    )
    return result.reshape(3, rows_x, rows_z, rows_y)


def local(
    velocity,
    point_velocity,
    point_coef,
    point_width,
    send_point,
    send_count,
    slot_offset,
    send_anchor,
    vertical_inverse,
):
    rows_x = velocity.shape[1]
    rows_z = velocity.shape[2]
    rows_y = velocity.shape[3]
    slot_total = send_point.shape[1]
    device_count = lax.axis_size("gx") * lax.axis_size("gy")
    capacity = slot_total // device_count
    records = source_records(
        point_velocity,
        point_coef[None, :],
        point_width[None, :],
        send_point,
        send_count,
        slot_offset,
    )
    fields = records.shape[1] // capacity
    arrived = lax.all_to_all(records, ("gx", "gy"), split_axis=0, concat_axis=0, tiled=True)
    arrived = arrived.reshape(device_count, fields, capacity).transpose(1, 0, 2)
    arrived = arrived.reshape(fields, slot_total)
    anchors = send_anchor[0]
    corner_x = anchors // (rows_z * rows_y)
    remainder = anchors % (rows_z * rows_y)
    corner_z = remainder // rows_y
    corner_y = remainder % rows_y
    forcing = deposit_blocks(arrived, corner_x, corner_z, corner_y, rows_x, rows_z, rows_y, K)
    wide_x = with_halo(velocity, (("gy", 1),), 1, True)
    grad_x = (wide_x[:, 2:] - wide_x[:, :-2]) * 0.5
    grad_y = (jnp.roll(velocity, -1, axis=3) - jnp.roll(velocity, 1, axis=3)) * 0.5
    flat_part = velocity[0:1] * grad_x + velocity[1:2] * grad_y
    inner = jnp.pad(velocity, ((0, 0), (0, 0), (1, 1), (0, 0)))
    inner_grad_z = (inner[:, :, 2:] - inner[:, :, :-2]) * 0.5
    partial = velocity + time_step * (forcing - flat_part)
    partial = partial - time_step * (velocity[2:3] * inner_grad_z)
    half = rows_z // 2
    edges = jnp.concatenate([velocity[:, :, :1], velocity[:, :, -1:]], axis=2)
    packed = jnp.concatenate([partial[:, :, :half], partial[:, :, half:], edges], axis=0)
    packed = lax.all_to_all(packed, "gx", split_axis=1, concat_axis=2, tiled=True)
    levels = lax.axis_size("gx")
    packed = packed.reshape(packed.shape[0], 1, levels, 2, rows_y)
    part = jnp.concatenate([packed[0:3], packed[3:6]], axis=3)
    edge = packed[6:9]
    below = jnp.pad(edge[:, :, :-1, 1], ((0, 0), (0, 0), (1, 0), (0, 0)))
    above = jnp.pad(edge[:, :, 1:, 0], ((0, 0), (0, 0), (0, 1), (0, 0)))
    first = part[:, :, :, 0] + time_step * (edge[2:3, :, :, 0] * (below * 0.5))
    last = part[:, :, :, -1] - time_step * (edge[2:3, :, :, 1] * (above * 0.5))
    columns = jnp.concatenate([first[:, :, :, None], part[:, :, :, 1:-1], last[:, :, :, None]], axis=3)
    columns = columns.reshape(3, 1, levels * rows_z, rows_y)
    solved = jnp.einsum("zk,cxky->cxzy", vertical_inverse, columns, precision=lax.Precision.HIGHEST)
    solved = solved.reshape(3, rows_x, rows_z, rows_y)
    new_velocity = lax.all_to_all(solved, "gx", split_axis=1, concat_axis=1, tiled=True)
    return new_velocity


def solution(mesh):
    placed = (
        P(None, "gy", "gx", None),
        P(None, ("gx", "gy")),
        P(("gx", "gy")),
        P(("gx", "gy")),
        P(("gx", "gy"), None),
        P(("gx", "gy"), None),
        P(None, ("gx", "gy"), None),
        P(("gx", "gy"), None),
        P(),
    )

    return jax.shard_map(
        local, mesh=mesh, in_specs=placed, out_specs=P(None, "gy", "gx", None), check_vma=False
    )
```

```python
import math

import jax
import jax.numpy as jnp
from jax import lax
from jax.experimental import pallas as pl
from jax.sharding import PartitionSpec as P


def _rows(pieces, shape):
    row = lax.broadcasted_iota(jnp.int32, shape, 0)
    total = jnp.zeros(shape, jnp.float32)
    for k, piece in enumerate(pieces):
        total = jnp.where(row == k, jnp.broadcast_to(piece, shape), total)
    return total


def _pieces(x):
    high = x.astype(jnp.bfloat16)
    rest = x - high.astype(jnp.float32)
    middle = rest.astype(jnp.bfloat16)
    low = (rest - middle.astype(jnp.float32)).astype(jnp.bfloat16)
    return high, middle, low


def _exact_dot(values, pick, dims):
    rows = values.shape[0]
    stacked = jnp.concatenate(_pieces(values), axis=0)
    term = lax.dot_general(stacked, pick, dims, preferred_element_type=jnp.float32)
    return (term[:rows] + term[rows : 2 * rows]) + term[2 * rows :]


def source_kernel(pv_ref, coef_ref, width_ref, sp_ref, cnt_ref, off_ref, out_ref):
    points = pv_ref.shape[1]
    slots = sp_ref.shape[1]
    tiles = cnt_ref.shape[1]
    capacity = slots // tiles
    lanes_out = out_ref.shape[1]
    fields = lanes_out // capacity
    plain = (((1,), (0,)), ((), ()))
    pv = pv_ref[...]
    speed = jnp.sqrt(pv[0:1] * pv[0:1] + pv[1:2] * pv[1:2] + pv[2:3] * pv[2:3])
    force = -(coef_ref[...] * speed) * pv
    vals = _rows([force[0:1], force[1:2], force[2:3], width_ref[...]], (16, points))
    pick = (lax.broadcasted_iota(jnp.int32, (points, slots), 0) == sp_ref[...]).astype(jnp.bfloat16)
    picked = _exact_dot(vals, pick, plain)
    slot_at = lax.broadcasted_iota(jnp.int32, (tiles, slots), 1)
    tile_at = lax.broadcasted_iota(jnp.int32, (tiles, slots), 0)
    tile_of = (slot_at // capacity == tile_at).astype(jnp.bfloat16)
    counts = _rows([cnt_ref[...].astype(jnp.float32)], (8, tiles)).astype(jnp.bfloat16)
    limit = lax.dot_general(counts, tile_of, plain, preferred_element_type=jnp.float32)[0:1]
    lane = (lax.broadcasted_iota(jnp.int32, (1, slots), 1) % capacity).astype(jnp.float32)
    live = jnp.where(lane < limit, 1.0, 0.0)
    table = _rows([picked[0:1] * live, picked[1:2] * live, picked[2:3] * live,
                   off_ref[0, 0:1, :], off_ref[1, 0:1, :], off_ref[2, 0:1, :], picked[3:4]],
                  (fields, slots))
    spread = jnp.concatenate(
        [jnp.broadcast_to(table[v:v + 1], (capacity, slots)) for v in range(fields)], axis=0)
    same_c = (lax.broadcasted_iota(jnp.int32, (lanes_out, slots), 1) % capacity
              == lax.broadcasted_iota(jnp.int32, (lanes_out, slots), 0) % capacity)
    spread = jnp.where(same_c, spread, 0.0)
    slot_row = lax.broadcasted_iota(jnp.int32, (slots, tiles), 0)
    tile_col = lax.broadcasted_iota(jnp.int32, (slots, tiles), 1)
    slot_tile = (slot_row // capacity == tile_col).astype(jnp.bfloat16)
    out_ref[...] = _exact_dot(spread, slot_tile, plain).T


def source_records(pv, coef, width, sp, cnt, off):
    tiles = cnt.shape[1]
    capacity = sp.shape[1] // tiles
    return pl.pallas_call(
        source_kernel,
        out_shape=jax.ShapeDtypeStruct((tiles, 8 * capacity), jnp.float32),
    )(pv, coef, width, sp, cnt, off)


K = 4


time_step = 0.25


def with_halo(block, sides, width, periodic):
    for axis, dim in sides:
        count = lax.axis_size(axis)
        forward = [(i, i + 1) for i in range(count - 1)]
        if periodic:
            forward.append((count - 1, 0))
        backward = [(target, source) for source, target in forward]
        low = lax.ppermute(
            lax.slice_in_dim(block, block.shape[dim] - width, None, axis=dim), axis, forward
        )
        high = lax.ppermute(lax.slice_in_dim(block, 0, width, axis=dim), axis, backward)
        block = jnp.concatenate([low, block, high], axis=dim)
    return block


def block_factor(corner, offset, extent, inverse_square, block_edge):
    cells = jnp.arange(extent, dtype=jnp.int32)[:, None]
    shifted = cells - corner[None, :]
    inside = (shifted >= 0) & (shifted < block_edge)
    spread = shifted.astype(jnp.float32) + 0.5 - offset[None, :]
    return jnp.where(inside, jnp.exp(-(spread * spread) * inverse_square[None, :]), 0.0)


def deposit_blocks(arrived, corner_x, corner_z, corner_y, rows_x, rows_z, rows_y, block_edge):
    width = arrived[6]
    inverse_square = 1.0 / (width * width)
    scaled = arrived[0:3] / (math.pi**1.5 * width**3)[None, :]
    along_x = block_factor(corner_x, arrived[3], rows_x, inverse_square, block_edge)
    along_z = block_factor(corner_z, arrived[4], rows_z, inverse_square, block_edge)
    along_y = block_factor(corner_y, arrived[5], rows_y, inverse_square, block_edge)
    left = scaled[:, None, None, :] * along_x[None, :, None, :] * along_z[None, None, :, :]
    left = left.reshape(3 * rows_x * rows_z, -1)
    result = lax.dot_general(
        left,
        along_y,
        (((1,), (1,)), ((), ())),
        precision=lax.Precision.HIGH,
        preferred_element_type=jnp.float32,
    )
    return result.reshape(3, rows_x, rows_z, rows_y)


def local(
    velocity,
    point_velocity,
    point_coef,
    point_width,
    send_point,
    send_count,
    slot_offset,
    send_anchor,
    vertical_inverse,
):
    rows_x = velocity.shape[1]
    rows_z = velocity.shape[2]
    rows_y = velocity.shape[3]
    slot_total = send_point.shape[1]
    device_count = lax.axis_size("gx") * lax.axis_size("gy")
    capacity = slot_total // device_count
    records = source_records(
        point_velocity,
        point_coef[None, :],
        point_width[None, :],
        send_point,
        send_count,
        slot_offset,
    )
    fields = records.shape[1] // capacity
    arrived = lax.all_to_all(records, ("gx", "gy"), split_axis=0, concat_axis=0, tiled=True)
    arrived = arrived.reshape(device_count, fields, capacity).transpose(1, 0, 2)
    arrived = arrived.reshape(fields, slot_total)
    anchors = send_anchor[0]
    corner_x = anchors // (rows_z * rows_y)
    remainder = anchors % (rows_z * rows_y)
    corner_z = remainder // rows_y
    corner_y = remainder % rows_y
    forcing = deposit_blocks(arrived, corner_x, corner_z, corner_y, rows_x, rows_z, rows_y, K)
    wide_x = with_halo(velocity, (("gy", 1),), 1, True)
    grad_x = (wide_x[:, 2:] - wide_x[:, :-2]) * 0.5
    grad_y = (jnp.roll(velocity, -1, axis=3) - jnp.roll(velocity, 1, axis=3)) * 0.5
    flat_part = velocity[0:1] * grad_x + velocity[1:2] * grad_y
    partial = velocity + time_step * (forcing - flat_part)
    both = jnp.concatenate([velocity, partial], axis=0)
    columns = lax.all_to_all(both, "gx", split_axis=1, concat_axis=2, tiled=True)
    column_velocity = columns[0:3]
    padded = jnp.pad(column_velocity, ((0, 0), (0, 0), (1, 1), (0, 0)))
    grad_z = (padded[:, :, 2:] - padded[:, :, :-2]) * 0.5
    columns = columns[3:6] - time_step * (column_velocity[2:3] * grad_z)
    solved = jnp.einsum("zk,cxky->cxzy", vertical_inverse, columns, precision=lax.Precision.HIGHEST)
    solved = solved.reshape(3, rows_x, rows_z, rows_y)
    new_velocity = lax.all_to_all(solved, "gx", split_axis=1, concat_axis=1, tiled=True)
    return new_velocity


def solution(mesh):
    placed = (
        P(None, "gy", "gx", None),
        P(None, ("gx", "gy")),
        P(("gx", "gy")),
        P(("gx", "gy")),
        P(("gx", "gy"), None),
        P(("gx", "gy"), None),
        P(None, ("gx", "gy"), None),
        P(("gx", "gy"), None),
        P(),
    )

    return jax.shard_map(
        local, mesh=mesh, in_specs=placed, out_specs=P(None, "gy", "gx", None), check_vma=False
    )
```

```python
import math

import jax
import jax.numpy as jnp
from jax import lax
from jax.experimental import pallas as pl
from jax.sharding import PartitionSpec as P


def _rows(pieces, shape):
    row = lax.broadcasted_iota(jnp.int32, shape, 0)
    total = jnp.zeros(shape, jnp.float32)
    for k, piece in enumerate(pieces):
        total = jnp.where(row == k, jnp.broadcast_to(piece, shape), total)
    return total


def _pieces(x):
    high = x.astype(jnp.bfloat16)
    rest = x - high.astype(jnp.float32)
    middle = rest.astype(jnp.bfloat16)
    low = (rest - middle.astype(jnp.float32)).astype(jnp.bfloat16)
    return high, middle, low


def _exact_dot(values, pick, dims):
    rows = values.shape[0]
    stacked = jnp.concatenate(_pieces(values), axis=0)
    term = lax.dot_general(stacked, pick, dims, preferred_element_type=jnp.float32)
    return (term[:rows] + term[rows : 2 * rows]) + term[2 * rows :]


def source_kernel(pv_ref, coef_ref, width_ref, sp_ref, cnt_ref, off_ref, out_ref):
    points = pv_ref.shape[1]
    slots = sp_ref.shape[1]
    tiles = cnt_ref.shape[1]
    capacity = slots // tiles
    lanes_out = out_ref.shape[1]
    fields = lanes_out // capacity
    plain = (((1,), (0,)), ((), ()))
    pv = pv_ref[...]
    speed = jnp.sqrt(pv[0:1] * pv[0:1] + pv[1:2] * pv[1:2] + pv[2:3] * pv[2:3])
    force = -(coef_ref[...] * speed) * pv
    width = width_ref[...]
    force = force / (math.pi**1.5 * (width * width * width))
    vals = _rows([force[0:1], force[1:2], force[2:3], 1.0 / (width * width)], (16, points))
    pick = (lax.broadcasted_iota(jnp.int32, (points, slots), 0) == sp_ref[...]).astype(jnp.bfloat16)
    picked = _exact_dot(vals, pick, plain)
    slot_at = lax.broadcasted_iota(jnp.int32, (tiles, slots), 1)
    tile_at = lax.broadcasted_iota(jnp.int32, (tiles, slots), 0)
    tile_of = (slot_at // capacity == tile_at).astype(jnp.bfloat16)
    counts = _rows([cnt_ref[...].astype(jnp.float32)], (8, tiles)).astype(jnp.bfloat16)
    limit = lax.dot_general(counts, tile_of, plain, preferred_element_type=jnp.float32)[0:1]
    lane = (lax.broadcasted_iota(jnp.int32, (1, slots), 1) % capacity).astype(jnp.float32)
    live = jnp.where(lane < limit, 1.0, 0.0)
    table = _rows([picked[0:1] * live, picked[1:2] * live, picked[2:3] * live,
                   off_ref[0, 0:1, :], off_ref[1, 0:1, :], off_ref[2, 0:1, :], picked[3:4]],
                  (fields, slots))
    spread = jnp.concatenate(
        [jnp.broadcast_to(table[v:v + 1], (capacity, slots)) for v in range(fields)], axis=0)
    same_c = (lax.broadcasted_iota(jnp.int32, (lanes_out, slots), 1) % capacity
              == lax.broadcasted_iota(jnp.int32, (lanes_out, slots), 0) % capacity)
    spread = jnp.where(same_c, spread, 0.0)
    slot_row = lax.broadcasted_iota(jnp.int32, (slots, tiles), 0)
    tile_col = lax.broadcasted_iota(jnp.int32, (slots, tiles), 1)
    slot_tile = (slot_row // capacity == tile_col).astype(jnp.bfloat16)
    out_ref[...] = _exact_dot(spread, slot_tile, plain).T


def source_records(pv, coef, width, sp, cnt, off):
    tiles = cnt.shape[1]
    capacity = sp.shape[1] // tiles
    return pl.pallas_call(
        source_kernel,
        out_shape=jax.ShapeDtypeStruct((tiles, 8 * capacity), jnp.float32),
    )(pv, coef, width, sp, cnt, off)


K = 4


time_step = 0.25


def with_halo(block, sides, width, periodic):
    for axis, dim in sides:
        count = lax.axis_size(axis)
        forward = [(i, i + 1) for i in range(count - 1)]
        if periodic:
            forward.append((count - 1, 0))
        backward = [(target, source) for source, target in forward]
        low = lax.ppermute(
            lax.slice_in_dim(block, block.shape[dim] - width, None, axis=dim), axis, forward
        )
        high = lax.ppermute(lax.slice_in_dim(block, 0, width, axis=dim), axis, backward)
        block = jnp.concatenate([low, block, high], axis=dim)
    return block


def block_factor(corner, offset, extent, inverse_square, block_edge):
    cells = jnp.arange(extent, dtype=jnp.int32)[:, None]
    shifted = cells - corner[None, :]
    inside = (shifted >= 0) & (shifted < block_edge)
    spread = shifted.astype(jnp.float32) + 0.5 - offset[None, :]
    return jnp.where(inside, jnp.exp(-(spread * spread) * inverse_square[None, :]), 0.0)


def deposit_blocks(arrived, corner_x, corner_z, corner_y, rows_x, rows_z, rows_y, block_edge):
    inverse_square = arrived[6]
    scaled = arrived[0:3]
    along_x = block_factor(corner_x, arrived[3], rows_x, inverse_square, block_edge)
    along_z = block_factor(corner_z, arrived[4], rows_z, inverse_square, block_edge)
    along_y = block_factor(corner_y, arrived[5], rows_y, inverse_square, block_edge)
    left = scaled[:, None, None, :] * along_x[None, :, None, :] * along_z[None, None, :, :]
    left = left.reshape(3 * rows_x * rows_z, -1)
    result = lax.dot_general(
        left,
        along_y,
        (((1,), (1,)), ((), ())),
        precision=lax.Precision.HIGH,
        preferred_element_type=jnp.float32,
    )
    return result.reshape(3, rows_x, rows_z, rows_y)


def local(
    velocity,
    point_velocity,
    point_coef,
    point_width,
    send_point,
    send_count,
    slot_offset,
    send_anchor,
    vertical_inverse,
):
    rows_x = velocity.shape[1]
    rows_z = velocity.shape[2]
    rows_y = velocity.shape[3]
    slot_total = send_point.shape[1]
    device_count = lax.axis_size("gx") * lax.axis_size("gy")
    capacity = slot_total // device_count
    records = source_records(
        point_velocity,
        point_coef[None, :],
        point_width[None, :],
        send_point,
        send_count,
        slot_offset,
    )
    fields = records.shape[1] // capacity
    arrived = lax.all_to_all(records, ("gx", "gy"), split_axis=0, concat_axis=0, tiled=True)
    arrived = arrived.reshape(device_count, fields, capacity).transpose(1, 0, 2)
    arrived = arrived.reshape(fields, slot_total)
    anchors = send_anchor[0]
    corner_x = anchors // (rows_z * rows_y)
    remainder = anchors % (rows_z * rows_y)
    corner_z = remainder // rows_y
    corner_y = remainder % rows_y
    forcing = deposit_blocks(arrived, corner_x, corner_z, corner_y, rows_x, rows_z, rows_y, K)
    wide_x = with_halo(velocity, (("gy", 1),), 1, True)
    grad_x = (wide_x[:, 2:] - wide_x[:, :-2]) * 0.5
    grad_y = (jnp.roll(velocity, -1, axis=3) - jnp.roll(velocity, 1, axis=3)) * 0.5
    flat_part = velocity[0:1] * grad_x + velocity[1:2] * grad_y
    partial = velocity + time_step * (forcing - flat_part)
    both = jnp.concatenate([velocity, partial], axis=0)
    columns = lax.all_to_all(both, "gx", split_axis=1, concat_axis=2, tiled=True)
    column_velocity = columns[0:3]
    padded = jnp.pad(column_velocity, ((0, 0), (0, 0), (1, 1), (0, 0)))
    grad_z = (padded[:, :, 2:] - padded[:, :, :-2]) * 0.5
    columns = columns[3:6] - time_step * (column_velocity[2:3] * grad_z)
    solved = jnp.einsum("zk,cxky->cxzy", vertical_inverse, columns, precision=lax.Precision.HIGHEST)
    solved = solved.reshape(3, rows_x, rows_z, rows_y)
    new_velocity = lax.all_to_all(solved, "gx", split_axis=1, concat_axis=1, tiled=True)
    return new_velocity


def solution(mesh):
    placed = (
        P(None, "gy", "gx", None),
        P(None, ("gx", "gy")),
        P(("gx", "gy")),
        P(("gx", "gy")),
        P(("gx", "gy"), None),
        P(("gx", "gy"), None),
        P(None, ("gx", "gy"), None),
        P(("gx", "gy"), None),
        P(),
    )

    return jax.shard_map(
        local, mesh=mesh, in_specs=placed, out_specs=P(None, "gy", "gx", None), check_vma=False
    )
```

```python
import math

import jax
import jax.numpy as jnp
from jax import lax
from jax.experimental import pallas as pl
from jax.sharding import PartitionSpec as P


def _rows(pieces, shape):
    row = lax.broadcasted_iota(jnp.int32, shape, 0)
    total = jnp.zeros(shape, jnp.float32)
    for k, piece in enumerate(pieces):
        total = jnp.where(row == k, jnp.broadcast_to(piece, shape), total)
    return total


def _pieces(x):
    high = x.astype(jnp.bfloat16)
    rest = x - high.astype(jnp.float32)
    middle = rest.astype(jnp.bfloat16)
    low = (rest - middle.astype(jnp.float32)).astype(jnp.bfloat16)
    return high, middle, low


def _exact_dot(values, pick, dims):
    rows = values.shape[0]
    stacked = jnp.concatenate(_pieces(values), axis=0)
    term = lax.dot_general(stacked, pick, dims, preferred_element_type=jnp.float32)
    return (term[:rows] + term[rows : 2 * rows]) + term[2 * rows :]


def source_kernel(pv_ref, coef_ref, width_ref, sp_ref, cnt_ref, off_ref, out_ref):
    points = pv_ref.shape[1]
    slots = sp_ref.shape[1]
    tiles = cnt_ref.shape[1]
    capacity = slots // tiles
    lanes_out = out_ref.shape[1]
    fields = lanes_out // capacity
    plain = (((1,), (0,)), ((), ()))
    pv = pv_ref[...]
    speed = jnp.sqrt(pv[0:1] * pv[0:1] + pv[1:2] * pv[1:2] + pv[2:3] * pv[2:3])
    force = -(coef_ref[...] * speed) * pv
    vals = _rows([force[0:1], force[1:2], force[2:3], width_ref[...]], (16, points))
    pick = (lax.broadcasted_iota(jnp.int32, (points, slots), 0) == sp_ref[...]).astype(jnp.bfloat16)
    picked = _exact_dot(vals, pick, plain)
    slot_at = lax.broadcasted_iota(jnp.int32, (tiles, slots), 1)
    tile_at = lax.broadcasted_iota(jnp.int32, (tiles, slots), 0)
    tile_of = (slot_at // capacity == tile_at).astype(jnp.bfloat16)
    counts = _rows([cnt_ref[...].astype(jnp.float32)], (8, tiles)).astype(jnp.bfloat16)
    limit = lax.dot_general(counts, tile_of, plain, preferred_element_type=jnp.float32)[0:1]
    lane = (lax.broadcasted_iota(jnp.int32, (1, slots), 1) % capacity).astype(jnp.float32)
    live = jnp.where(lane < limit, 1.0, 0.0)
    table = _rows([picked[0:1] * live, picked[1:2] * live, picked[2:3] * live,
                   off_ref[0, 0:1, :], off_ref[1, 0:1, :], off_ref[2, 0:1, :], picked[3:4]],
                  (fields, slots))
    spread = jnp.concatenate(
        [jnp.broadcast_to(table[v:v + 1], (capacity, slots)) for v in range(fields)], axis=0)
    same_c = (lax.broadcasted_iota(jnp.int32, (lanes_out, slots), 1) % capacity
              == lax.broadcasted_iota(jnp.int32, (lanes_out, slots), 0) % capacity)
    spread = jnp.where(same_c, spread, 0.0)
    slot_row = lax.broadcasted_iota(jnp.int32, (slots, tiles), 0)
    tile_col = lax.broadcasted_iota(jnp.int32, (slots, tiles), 1)
    slot_tile = (slot_row // capacity == tile_col).astype(jnp.bfloat16)
    out_ref[...] = _exact_dot(spread, slot_tile, plain).T


def source_records(pv, coef, width, sp, cnt, off):
    tiles = cnt.shape[1]
    capacity = sp.shape[1] // tiles
    return pl.pallas_call(
        source_kernel,
        out_shape=jax.ShapeDtypeStruct((tiles, 8 * capacity), jnp.float32),
    )(pv, coef, width, sp, cnt, off)


K = 4


time_step = 0.25


def with_halo(block, sides, width, periodic):
    for axis, dim in sides:
        count = lax.axis_size(axis)
        forward = [(i, i + 1) for i in range(count - 1)]
        if periodic:
            forward.append((count - 1, 0))
        backward = [(target, source) for source, target in forward]
        low = lax.ppermute(
            lax.slice_in_dim(block, block.shape[dim] - width, None, axis=dim), axis, forward
        )
        high = lax.ppermute(lax.slice_in_dim(block, 0, width, axis=dim), axis, backward)
        block = jnp.concatenate([low, block, high], axis=dim)
    return block


def block_factor(corner, offset, extent, inverse_square, block_edge):
    cells = jnp.arange(extent, dtype=jnp.int32)[:, None]
    shifted = cells - corner[None, :]
    inside = (shifted >= 0) & (shifted < block_edge)
    spread = shifted.astype(jnp.float32) + 0.5 - offset[None, :]
    return jnp.where(inside, jnp.exp(-(spread * spread) * inverse_square[None, :]), 0.0)


def deposit_blocks(arrived, corner_x, corner_z, corner_y, rows_x, rows_z, rows_y, block_edge):
    width = arrived[6]
    inverse_square = 1.0 / (width * width)
    scaled = arrived[0:3] / (math.pi**1.5 * width**3)[None, :]
    along_x = block_factor(corner_x, arrived[3], rows_x, inverse_square, block_edge)
    along_z = block_factor(corner_z, arrived[4], rows_z, inverse_square, block_edge)
    along_y = block_factor(corner_y, arrived[5], rows_y, inverse_square, block_edge)
    left = scaled[:, None, None, :] * along_x[None, :, None, :] * along_z[None, None, :, :]
    left = left.reshape(3 * rows_x * rows_z, -1)
    result = lax.dot_general(
        left,
        along_y,
        (((1,), (1,)), ((), ())),
        precision=lax.Precision.HIGH,
        preferred_element_type=jnp.float32,
    )
    return result.reshape(3, rows_x, rows_z, rows_y)


def local(
    velocity,
    point_velocity,
    point_coef,
    point_width,
    send_point,
    send_count,
    slot_offset,
    send_anchor,
    vertical_inverse,
):
    rows_x = velocity.shape[1]
    rows_z = velocity.shape[2]
    rows_y = velocity.shape[3]
    slot_total = send_point.shape[1]
    device_count = lax.axis_size("gx") * lax.axis_size("gy")
    capacity = slot_total // device_count
    records = source_records(
        point_velocity,
        point_coef[None, :],
        point_width[None, :],
        send_point,
        send_count,
        slot_offset,
    )
    fields = records.shape[1] // capacity
    arrived = lax.all_to_all(records, ("gx", "gy"), split_axis=0, concat_axis=0, tiled=True)
    arrived = arrived.reshape(device_count, fields, capacity).transpose(1, 0, 2)
    arrived = arrived.reshape(fields, slot_total)
    anchors = send_anchor[0]
    corner_x = anchors // (rows_z * rows_y)
    remainder = anchors % (rows_z * rows_y)
    corner_z = remainder // rows_y
    corner_y = remainder % rows_y
    forcing = deposit_blocks(arrived, corner_x, corner_z, corner_y, rows_x, rows_z, rows_y, K)
    wide_x = with_halo(velocity, (("gy", 1),), 1, True)
    grad_x = (wide_x[:, 2:] - wide_x[:, :-2]) * 0.5
    grad_y = (jnp.roll(velocity, -1, axis=3) - jnp.roll(velocity, 1, axis=3)) * 0.5
    flat_part = velocity[0:1] * grad_x + velocity[1:2] * grad_y
    inner = jnp.pad(velocity, ((0, 0), (0, 0), (1, 1), (0, 0)))
    inner_grad_z = (inner[:, :, 2:] - inner[:, :, :-2]) * 0.5
    partial = velocity + time_step * (forcing - flat_part)
    partial = partial - time_step * (velocity[2:3] * inner_grad_z)
    edges = jnp.concatenate([velocity[:, :, :1], velocity[:, :, -1:]], axis=2)
    edges = edges.reshape(3, rows_x, rows_z, 2 * rows_y // rows_z)
    packed = jnp.concatenate([partial, edges], axis=3)
    packed = lax.all_to_all(packed, "gx", split_axis=1, concat_axis=2, tiled=True)
    levels = lax.axis_size("gx")
    part = packed[..., :rows_y].reshape(3, 1, levels, rows_z, rows_y)
    edge = packed[..., rows_y:].reshape(3, 1, levels, 2, rows_y)
    below = jnp.pad(edge[:, :, :-1, 1], ((0, 0), (0, 0), (1, 0), (0, 0)))
    above = jnp.pad(edge[:, :, 1:, 0], ((0, 0), (0, 0), (0, 1), (0, 0)))
    first = part[:, :, :, 0] + time_step * (edge[2:3, :, :, 0] * (below * 0.5))
    last = part[:, :, :, -1] - time_step * (edge[2:3, :, :, 1] * (above * 0.5))
    columns = jnp.concatenate([first[:, :, :, None], part[:, :, :, 1:-1], last[:, :, :, None]], axis=3)
    columns = columns.reshape(3, 1, levels * rows_z, rows_y)
    solved = jnp.einsum("zk,cxky->cxzy", vertical_inverse, columns, precision=lax.Precision.HIGHEST)
    solved = solved.reshape(3, rows_x, rows_z, rows_y)
    new_velocity = lax.all_to_all(solved, "gx", split_axis=1, concat_axis=1, tiled=True)
    return new_velocity


def solution(mesh):
    placed = (
        P(None, "gy", "gx", None),
        P(None, ("gx", "gy")),
        P(("gx", "gy")),
        P(("gx", "gy")),
        P(("gx", "gy"), None),
        P(("gx", "gy"), None),
        P(None, ("gx", "gy"), None),
        P(("gx", "gy"), None),
        P(),
    )

    return jax.shard_map(
        local, mesh=mesh, in_specs=placed, out_specs=P(None, "gy", "gx", None), check_vma=False
    )
```

```python
import functools
import math

import jax
import jax.numpy as jnp
from jax import lax
from jax.experimental import pallas as pl
from jax.sharding import PartitionSpec as P


def _rows(pieces, shape):
    row = lax.broadcasted_iota(jnp.int32, shape, 0)
    total = jnp.zeros(shape, jnp.float32)
    for k, piece in enumerate(pieces):
        total = jnp.where(row == k, jnp.broadcast_to(piece, shape), total)
    return total


def _pieces(x):
    high = x.astype(jnp.bfloat16)
    rest = x - high.astype(jnp.float32)
    middle = rest.astype(jnp.bfloat16)
    low = (rest - middle.astype(jnp.float32)).astype(jnp.bfloat16)
    return high, middle, low


def _exact_dot(values, pick, dims):
    rows = values.shape[0]
    stacked = jnp.concatenate(_pieces(values), axis=0)
    term = lax.dot_general(stacked, pick, dims, preferred_element_type=jnp.float32)
    return (term[:rows] + term[rows : 2 * rows]) + term[2 * rows :]


def source_kernel(pv_ref, coef_ref, width_ref, sp_ref, cnt_ref, off_ref, out_ref, *, major):
    points = pv_ref.shape[1]
    slots = sp_ref.shape[1]
    tiles = cnt_ref.shape[1]
    capacity = slots // tiles
    lanes_out = out_ref.shape[1]
    fields = lanes_out // capacity
    plain = (((1,), (0,)), ((), ()))
    pv = pv_ref[...]
    speed = jnp.sqrt(pv[0:1] * pv[0:1] + pv[1:2] * pv[1:2] + pv[2:3] * pv[2:3])
    force = -(coef_ref[...] * speed) * pv
    vals = _rows([force[0:1], force[1:2], force[2:3], width_ref[...]], (16, points))
    pick = (lax.broadcasted_iota(jnp.int32, (points, slots), 0) == sp_ref[...]).astype(jnp.bfloat16)
    picked = _exact_dot(vals, pick, plain)
    slot_at = lax.broadcasted_iota(jnp.int32, (tiles, slots), 1)
    tile_at = lax.broadcasted_iota(jnp.int32, (tiles, slots), 0)
    tile_of = (slot_at // capacity == tile_at).astype(jnp.bfloat16)
    counts = _rows([cnt_ref[...].astype(jnp.float32)], (8, tiles)).astype(jnp.bfloat16)
    limit = lax.dot_general(counts, tile_of, plain, preferred_element_type=jnp.float32)[0:1]
    lane = (lax.broadcasted_iota(jnp.int32, (1, slots), 1) % capacity).astype(jnp.float32)
    live = jnp.where(lane < limit, 1.0, 0.0)
    table = _rows([picked[0:1] * live, picked[1:2] * live, picked[2:3] * live,
                   off_ref[0, 0:1, :], off_ref[1, 0:1, :], off_ref[2, 0:1, :], picked[3:4]],
                  (fields, slots))
    spread = jnp.concatenate(
        [jnp.broadcast_to(table[v:v + 1], (capacity, slots)) for v in range(fields)], axis=0)
    same_c = (lax.broadcasted_iota(jnp.int32, (lanes_out, slots), 1) % capacity
              == lax.broadcasted_iota(jnp.int32, (lanes_out, slots), 0) % capacity)
    spread = jnp.where(same_c, spread, 0.0)
    slot_row = lax.broadcasted_iota(jnp.int32, (slots, tiles), 0)
    tile_col = lax.broadcasted_iota(jnp.int32, (slots, tiles), 1)
    minor = tiles // major
    tile_col = (tile_col % major) * minor + tile_col // major
    slot_tile = (slot_row // capacity == tile_col).astype(jnp.bfloat16)
    out_ref[...] = _exact_dot(spread, slot_tile, plain).T


def source_records(pv, coef, width, sp, cnt, off, major):
    tiles = cnt.shape[1]
    capacity = sp.shape[1] // tiles
    return pl.pallas_call(
        functools.partial(source_kernel, major=major),
        out_shape=jax.ShapeDtypeStruct((tiles, 8 * capacity), jnp.float32),
    )(pv, coef, width, sp, cnt, off)


K = 4


time_step = 0.25


def with_halo(block, sides, width, periodic):
    for axis, dim in sides:
        count = lax.axis_size(axis)
        forward = [(i, i + 1) for i in range(count - 1)]
        if periodic:
            forward.append((count - 1, 0))
        backward = [(target, source) for source, target in forward]
        low = lax.ppermute(
            lax.slice_in_dim(block, block.shape[dim] - width, None, axis=dim), axis, forward
        )
        high = lax.ppermute(lax.slice_in_dim(block, 0, width, axis=dim), axis, backward)
        block = jnp.concatenate([low, block, high], axis=dim)
    return block


def block_factor(corner, offset, extent, inverse_square, block_edge):
    cells = jnp.arange(extent, dtype=jnp.int32)[:, None]
    shifted = cells - corner[None, :]
    inside = (shifted >= 0) & (shifted < block_edge)
    spread = shifted.astype(jnp.float32) + 0.5 - offset[None, :]
    return jnp.where(inside, jnp.exp(-(spread * spread) * inverse_square[None, :]), 0.0)


def deposit_blocks(arrived, corner_x, corner_z, corner_y, rows_x, rows_z, rows_y, block_edge):
    width = arrived[6]
    inverse_square = 1.0 / (width * width)
    scaled = arrived[0:3] / (math.pi**1.5 * width**3)[None, :]
    along_x = block_factor(corner_x, arrived[3], rows_x, inverse_square, block_edge)
    along_z = block_factor(corner_z, arrived[4], rows_z, inverse_square, block_edge)
    along_y = block_factor(corner_y, arrived[5], rows_y, inverse_square, block_edge)
    left = scaled[:, None, None, :] * along_x[None, :, None, :] * along_z[None, None, :, :]
    left = left.reshape(3 * rows_x * rows_z, -1)
    result = lax.dot_general(
        left,
        along_y,
        (((1,), (1,)), ((), ())),
        precision=lax.Precision.HIGH,
        preferred_element_type=jnp.float32,
    )
    return result.reshape(3, rows_x, rows_z, rows_y)


def local(
    velocity,
    point_velocity,
    point_coef,
    point_width,
    send_point,
    send_count,
    slot_offset,
    send_anchor,
    vertical_inverse,
):
    rows_x = velocity.shape[1]
    rows_z = velocity.shape[2]
    rows_y = velocity.shape[3]
    slot_total = send_point.shape[1]
    device_count = lax.axis_size("gx") * lax.axis_size("gy")
    capacity = slot_total // device_count
    records = source_records(
        point_velocity,
        point_coef[None, :],
        point_width[None, :],
        send_point,
        send_count,
        slot_offset,
        lax.axis_size("gx"),
    )
    fields = records.shape[1] // capacity
    arrived = lax.all_to_all(records, ("gy", "gx"), split_axis=0, concat_axis=0, tiled=True)
    arrived = arrived.reshape(device_count, fields, capacity).transpose(1, 0, 2)
    arrived = arrived.reshape(fields, slot_total)
    anchors = send_anchor.reshape(lax.axis_size("gx"), lax.axis_size("gy"), capacity)
    anchors = anchors.transpose(1, 0, 2).reshape(slot_total)
    corner_x = anchors // (rows_z * rows_y)
    remainder = anchors % (rows_z * rows_y)
    corner_z = remainder // rows_y
    corner_y = remainder % rows_y
    forcing = deposit_blocks(arrived, corner_x, corner_z, corner_y, rows_x, rows_z, rows_y, K)
    wide_x = with_halo(velocity, (("gy", 1),), 1, True)
    grad_x = (wide_x[:, 2:] - wide_x[:, :-2]) * 0.5
    grad_y = (jnp.roll(velocity, -1, axis=3) - jnp.roll(velocity, 1, axis=3)) * 0.5
    flat_part = velocity[0:1] * grad_x + velocity[1:2] * grad_y
    partial = velocity + time_step * (forcing - flat_part)
    both = jnp.concatenate([velocity, partial], axis=0)
    columns = lax.all_to_all(both, "gx", split_axis=1, concat_axis=2, tiled=True)
    column_velocity = columns[0:3]
    padded = jnp.pad(column_velocity, ((0, 0), (0, 0), (1, 1), (0, 0)))
    grad_z = (padded[:, :, 2:] - padded[:, :, :-2]) * 0.5
    columns = columns[3:6] - time_step * (column_velocity[2:3] * grad_z)
    solved = jnp.einsum("zk,cxky->cxzy", vertical_inverse, columns, precision=lax.Precision.HIGHEST)
    solved = solved.reshape(3, rows_x, rows_z, rows_y)
    new_velocity = lax.all_to_all(solved, "gx", split_axis=1, concat_axis=1, tiled=True)
    return new_velocity


def solution(mesh):
    placed = (
        P(None, "gy", "gx", None),
        P(None, ("gx", "gy")),
        P(("gx", "gy")),
        P(("gx", "gy")),
        P(("gx", "gy"), None),
        P(("gx", "gy"), None),
        P(None, ("gx", "gy"), None),
        P(("gx", "gy"), None),
        P(),
    )

    return jax.shard_map(
        local, mesh=mesh, in_specs=placed, out_specs=P(None, "gy", "gx", None), check_vma=False
    )
```

```python
import math

import jax
import jax.numpy as jnp
from jax import lax
from jax.experimental import pallas as pl
from jax.sharding import PartitionSpec as P


def _rows(pieces, shape):
    row = lax.broadcasted_iota(jnp.int32, shape, 0)
    total = jnp.zeros(shape, jnp.float32)
    for k, piece in enumerate(pieces):
        total = jnp.where(row == k, jnp.broadcast_to(piece, shape), total)
    return total


def _pieces(x):
    high = x.astype(jnp.bfloat16)
    rest = x - high.astype(jnp.float32)
    middle = rest.astype(jnp.bfloat16)
    low = (rest - middle.astype(jnp.float32)).astype(jnp.bfloat16)
    return high, middle, low


def _exact_dot(values, pick, dims):
    rows = values.shape[0]
    stacked = jnp.concatenate(_pieces(values), axis=0)
    term = lax.dot_general(stacked, pick, dims, preferred_element_type=jnp.float32)
    return (term[:rows] + term[rows : 2 * rows]) + term[2 * rows :]


def source_kernel(pv_ref, coef_ref, width_ref, sp_ref, cnt_ref, off_ref, out_ref):
    points = pv_ref.shape[1]
    slots = sp_ref.shape[1]
    tiles = cnt_ref.shape[1]
    capacity = slots // tiles
    lanes_out = out_ref.shape[1]
    fields = lanes_out // capacity
    plain = (((1,), (0,)), ((), ()))
    pv = pv_ref[...]
    speed = jnp.sqrt(pv[0:1] * pv[0:1] + pv[1:2] * pv[1:2] + pv[2:3] * pv[2:3])
    force = -(coef_ref[...] * speed) * pv
    width = width_ref[...]
    force = force / (math.pi**1.5 * (width * width * width))
    vals = _rows([force[0:1], force[1:2], force[2:3], 1.0 / (width * width)], (16, points))
    pick = (lax.broadcasted_iota(jnp.int32, (points, slots), 0) == sp_ref[...]).astype(jnp.bfloat16)
    picked = _exact_dot(vals, pick, plain)
    slot_at = lax.broadcasted_iota(jnp.int32, (tiles, slots), 1)
    tile_at = lax.broadcasted_iota(jnp.int32, (tiles, slots), 0)
    tile_of = (slot_at // capacity == tile_at).astype(jnp.bfloat16)
    counts = _rows([cnt_ref[...].astype(jnp.float32)], (8, tiles)).astype(jnp.bfloat16)
    limit = lax.dot_general(counts, tile_of, plain, preferred_element_type=jnp.float32)[0:1]
    lane = (lax.broadcasted_iota(jnp.int32, (1, slots), 1) % capacity).astype(jnp.float32)
    live = jnp.where(lane < limit, 1.0, 0.0)
    table = _rows([picked[0:1] * live, picked[1:2] * live, picked[2:3] * live,
                   off_ref[0, 0:1, :], off_ref[1, 0:1, :], off_ref[2, 0:1, :], picked[3:4]],
                  (fields, slots))
    spread = jnp.concatenate(
        [jnp.broadcast_to(table[v:v + 1], (capacity, slots)) for v in range(fields)], axis=0)
    same_c = (lax.broadcasted_iota(jnp.int32, (lanes_out, slots), 1) % capacity
              == lax.broadcasted_iota(jnp.int32, (lanes_out, slots), 0) % capacity)
    spread = jnp.where(same_c, spread, 0.0)
    slot_row = lax.broadcasted_iota(jnp.int32, (slots, tiles), 0)
    tile_col = lax.broadcasted_iota(jnp.int32, (slots, tiles), 1)
    slot_tile = (slot_row // capacity == tile_col).astype(jnp.bfloat16)
    out_ref[...] = _exact_dot(spread, slot_tile, plain).T


def source_records(pv, coef, width, sp, cnt, off):
    tiles = cnt.shape[1]
    capacity = sp.shape[1] // tiles
    return pl.pallas_call(
        source_kernel,
        out_shape=jax.ShapeDtypeStruct((tiles, 8 * capacity), jnp.float32),
    )(pv, coef, width, sp, cnt, off)


K = 4


time_step = 0.25


def with_halo(block, sides, width, periodic):
    for axis, dim in sides:
        count = lax.axis_size(axis)
        forward = [(i, i + 1) for i in range(count - 1)]
        if periodic:
            forward.append((count - 1, 0))
        backward = [(target, source) for source, target in forward]
        low = lax.ppermute(
            lax.slice_in_dim(block, block.shape[dim] - width, None, axis=dim), axis, forward
        )
        high = lax.ppermute(lax.slice_in_dim(block, 0, width, axis=dim), axis, backward)
        block = jnp.concatenate([low, block, high], axis=dim)
    return block


def block_factor(corner, offset, extent, inverse_square, block_edge):
    steps = jnp.arange(block_edge, dtype=jnp.int32)[:, None]
    spread = steps.astype(jnp.float32) + 0.5 - offset[None, :]
    values = jnp.exp(-(spread * spread) * inverse_square[None, :])
    shifted = jnp.arange(extent, dtype=jnp.int32)[:, None] - corner[None, :]
    result = jnp.zeros((extent, corner.shape[0]), jnp.float32)
    for step in range(block_edge):
        result = jnp.where(shifted == step, values[step][None, :], result)
    return result


def deposit_blocks(arrived, corner_x, corner_z, corner_y, rows_x, rows_z, rows_y, block_edge):
    inverse_square = arrived[6]
    scaled = arrived[0:3]
    along_x = block_factor(corner_x, arrived[3], rows_x, inverse_square, block_edge)
    along_z = block_factor(corner_z, arrived[4], rows_z, inverse_square, block_edge)
    along_y = block_factor(corner_y, arrived[5], rows_y, inverse_square, block_edge)
    left = scaled[:, None, None, :] * along_x[None, :, None, :] * along_z[None, None, :, :]
    left = left.reshape(3 * rows_x * rows_z, -1)
    result = lax.dot_general(
        left,
        along_y,
        (((1,), (1,)), ((), ())),
        precision=lax.Precision.HIGH,
        preferred_element_type=jnp.float32,
    )
    return result.reshape(3, rows_x, rows_z, rows_y)


def local(
    velocity,
    point_velocity,
    point_coef,
    point_width,
    send_point,
    send_count,
    slot_offset,
    send_anchor,
    vertical_inverse,
):
    rows_x = velocity.shape[1]
    rows_z = velocity.shape[2]
    rows_y = velocity.shape[3]
    slot_total = send_point.shape[1]
    device_count = lax.axis_size("gx") * lax.axis_size("gy")
    capacity = slot_total // device_count
    records = source_records(
        point_velocity,
        point_coef[None, :],
        point_width[None, :],
        send_point,
        send_count,
        slot_offset,
    )
    fields = records.shape[1] // capacity
    arrived = lax.all_to_all(records, ("gx", "gy"), split_axis=0, concat_axis=0, tiled=True)
    arrived = arrived.reshape(device_count, fields, capacity).transpose(1, 0, 2)
    arrived = arrived.reshape(fields, slot_total)
    anchors = send_anchor[0]
    corner_x = anchors // (rows_z * rows_y)
    remainder = anchors % (rows_z * rows_y)
    corner_z = remainder // rows_y
    corner_y = remainder % rows_y
    forcing = deposit_blocks(arrived, corner_x, corner_z, corner_y, rows_x, rows_z, rows_y, K)
    wide_x = with_halo(velocity, (("gy", 1),), 1, True)
    grad_x = (wide_x[:, 2:] - wide_x[:, :-2]) * 0.5
    grad_y = (jnp.roll(velocity, -1, axis=3) - jnp.roll(velocity, 1, axis=3)) * 0.5
    flat_part = velocity[0:1] * grad_x + velocity[1:2] * grad_y
    partial = velocity + time_step * (forcing - flat_part)
    both = jnp.concatenate([velocity, partial], axis=0)
    columns = lax.all_to_all(both, "gx", split_axis=1, concat_axis=2, tiled=True)
    column_velocity = columns[0:3]
    padded = jnp.pad(column_velocity, ((0, 0), (0, 0), (1, 1), (0, 0)))
    grad_z = (padded[:, :, 2:] - padded[:, :, :-2]) * 0.5
    columns = columns[3:6] - time_step * (column_velocity[2:3] * grad_z)
    solved = jnp.einsum("zk,cxky->cxzy", vertical_inverse, columns, precision=lax.Precision.HIGHEST)
    solved = solved.reshape(3, rows_x, rows_z, rows_y)
    new_velocity = lax.all_to_all(solved, "gx", split_axis=1, concat_axis=1, tiled=True)
    return new_velocity


def solution(mesh):
    placed = (
        P(None, "gy", "gx", None),
        P(None, ("gx", "gy")),
        P(("gx", "gy")),
        P(("gx", "gy")),
        P(("gx", "gy"), None),
        P(("gx", "gy"), None),
        P(None, ("gx", "gy"), None),
        P(("gx", "gy"), None),
        P(),
    )

    return jax.shard_map(
        local, mesh=mesh, in_specs=placed, out_specs=P(None, "gy", "gx", None), check_vma=False
    )
```

```python
import math

import jax
import jax.numpy as jnp
from jax import lax
from jax.experimental import pallas as pl
from jax.sharding import PartitionSpec as P


def _rows(pieces, shape):
    row = lax.broadcasted_iota(jnp.int32, shape, 0)
    total = jnp.zeros(shape, jnp.float32)
    for k, piece in enumerate(pieces):
        total = jnp.where(row == k, jnp.broadcast_to(piece, shape), total)
    return total


def _pieces(x):
    high = x.astype(jnp.bfloat16)
    rest = x - high.astype(jnp.float32)
    middle = rest.astype(jnp.bfloat16)
    low = (rest - middle.astype(jnp.float32)).astype(jnp.bfloat16)
    return high, middle, low


def _exact_dot(values, pick, dims):
    rows = values.shape[0]
    stacked = jnp.concatenate(_pieces(values), axis=0)
    term = lax.dot_general(stacked, pick, dims, preferred_element_type=jnp.float32)
    return (term[:rows] + term[rows : 2 * rows]) + term[2 * rows :]


def source_kernel(pv_ref, coef_ref, width_ref, sp_ref, cnt_ref, off_ref, out_ref):
    points = pv_ref.shape[1]
    slots = sp_ref.shape[1]
    tiles = cnt_ref.shape[1]
    capacity = slots // tiles
    lanes_out = out_ref.shape[1]
    fields = lanes_out // capacity
    plain = (((1,), (0,)), ((), ()))
    pv = pv_ref[...]
    speed = jnp.sqrt(pv[0:1] * pv[0:1] + pv[1:2] * pv[1:2] + pv[2:3] * pv[2:3])
    force = -(coef_ref[...] * speed) * pv
    vals = _rows([force[0:1], force[1:2], force[2:3], width_ref[...]], (16, points))
    pick = (lax.broadcasted_iota(jnp.int32, (points, slots), 0) == sp_ref[...]).astype(jnp.bfloat16)
    picked = _exact_dot(vals, pick, plain)
    slot_at = lax.broadcasted_iota(jnp.int32, (tiles, slots), 1)
    tile_at = lax.broadcasted_iota(jnp.int32, (tiles, slots), 0)
    tile_of = (slot_at // capacity == tile_at).astype(jnp.bfloat16)
    counts = _rows([cnt_ref[...].astype(jnp.float32)], (8, tiles)).astype(jnp.bfloat16)
    limit = lax.dot_general(counts, tile_of, plain, preferred_element_type=jnp.float32)[0:1]
    lane = (lax.broadcasted_iota(jnp.int32, (1, slots), 1) % capacity).astype(jnp.float32)
    live = jnp.where(lane < limit, 1.0, 0.0)
    table = _rows([picked[0:1] * live, picked[1:2] * live, picked[2:3] * live,
                   off_ref[0, 0:1, :], off_ref[1, 0:1, :], off_ref[2, 0:1, :], picked[3:4]],
                  (fields, slots))
    spread = jnp.concatenate(
        [jnp.broadcast_to(table[v:v + 1], (capacity, slots)) for v in range(fields)], axis=0)
    same_c = (lax.broadcasted_iota(jnp.int32, (lanes_out, slots), 1) % capacity
              == lax.broadcasted_iota(jnp.int32, (lanes_out, slots), 0) % capacity)
    spread = jnp.where(same_c, spread, 0.0)
    slot_row = lax.broadcasted_iota(jnp.int32, (slots, tiles), 0)
    tile_col = lax.broadcasted_iota(jnp.int32, (slots, tiles), 1)
    slot_tile = (slot_row // capacity == tile_col).astype(jnp.bfloat16)
    out_ref[...] = _exact_dot(spread, slot_tile, plain).T


def source_records(pv, coef, width, sp, cnt, off):
    tiles = cnt.shape[1]
    capacity = sp.shape[1] // tiles
    return pl.pallas_call(
        source_kernel,
        out_shape=jax.ShapeDtypeStruct((tiles, 8 * capacity), jnp.float32),
    )(pv, coef, width, sp, cnt, off)


K = 4


time_step = 0.25


def with_halo(block, sides, width, periodic):
    for axis, dim in sides:
        count = lax.axis_size(axis)
        forward = [(i, i + 1) for i in range(count - 1)]
        if periodic:
            forward.append((count - 1, 0))
        backward = [(target, source) for source, target in forward]
        low = lax.ppermute(
            lax.slice_in_dim(block, block.shape[dim] - width, None, axis=dim), axis, forward
        )
        high = lax.ppermute(lax.slice_in_dim(block, 0, width, axis=dim), axis, backward)
        block = jnp.concatenate([low, block, high], axis=dim)
    return block


def block_factor(corner, offset, extent, inverse_square, block_edge):
    steps = jnp.arange(block_edge, dtype=jnp.int32)[:, None]
    spread = steps.astype(jnp.float32) + 0.5 - offset[None, :]
    values = jnp.exp(-(spread * spread) * inverse_square[None, :])
    shifted = jnp.arange(extent, dtype=jnp.int32)[:, None] - corner[None, :]
    result = jnp.zeros((extent, corner.shape[0]), jnp.float32)
    for step in range(block_edge):
        result = jnp.where(shifted == step, values[step][None, :], result)
    return result


def deposit_blocks(arrived, corner_x, corner_z, corner_y, rows_x, rows_z, rows_y, block_edge):
    width = arrived[6]
    inverse_square = 1.0 / (width * width)
    scaled = arrived[0:3] / (math.pi**1.5 * width**3)[None, :]
    along_x = block_factor(corner_x, arrived[3], rows_x, inverse_square, block_edge)
    if rows_z == block_edge:
        levels = jnp.arange(rows_z, dtype=jnp.float32)[:, None] + 0.5 - arrived[4][None, :]
        along_z = jnp.exp(-(levels * levels) * inverse_square[None, :])
    else:
        along_z = block_factor(corner_z, arrived[4], rows_z, inverse_square, block_edge)
    along_y = block_factor(corner_y, arrived[5], rows_y, inverse_square, block_edge)
    left = scaled[:, None, None, :] * along_x[None, :, None, :] * along_z[None, None, :, :]
    left = left.reshape(3 * rows_x * rows_z, -1)
    result = lax.dot_general(
        left,
        along_y,
        (((1,), (1,)), ((), ())),
        precision=lax.Precision.HIGH,
        preferred_element_type=jnp.float32,
    )
    return result.reshape(3, rows_x, rows_z, rows_y)


def local(
    velocity,
    point_velocity,
    point_coef,
    point_width,
    send_point,
    send_count,
    slot_offset,
    send_anchor,
    vertical_inverse,
):
    rows_x = velocity.shape[1]
    rows_z = velocity.shape[2]
    rows_y = velocity.shape[3]
    slot_total = send_point.shape[1]
    device_count = lax.axis_size("gx") * lax.axis_size("gy")
    capacity = slot_total // device_count
    records = source_records(
        point_velocity,
        point_coef[None, :],
        point_width[None, :],
        send_point,
        send_count,
        slot_offset,
    )
    fields = records.shape[1] // capacity
    arrived = lax.all_to_all(records, ("gx", "gy"), split_axis=0, concat_axis=0, tiled=True)
    arrived = arrived.reshape(device_count, fields, capacity).transpose(1, 0, 2)
    arrived = arrived.reshape(fields, slot_total)
    anchors = send_anchor[0]
    corner_x = anchors // (rows_z * rows_y)
    remainder = anchors % (rows_z * rows_y)
    corner_z = remainder // rows_y
    corner_y = remainder % rows_y
    forcing = deposit_blocks(arrived, corner_x, corner_z, corner_y, rows_x, rows_z, rows_y, K)
    wide_x = with_halo(velocity, (("gy", 1),), 1, True)
    grad_x = (wide_x[:, 2:] - wide_x[:, :-2]) * 0.5
    grad_y = (jnp.roll(velocity, -1, axis=3) - jnp.roll(velocity, 1, axis=3)) * 0.5
    flat_part = velocity[0:1] * grad_x + velocity[1:2] * grad_y
    partial = velocity + time_step * (forcing - flat_part)
    both = jnp.concatenate([velocity, partial], axis=0)
    columns = lax.all_to_all(both, "gx", split_axis=1, concat_axis=2, tiled=True)
    column_velocity = columns[0:3]
    padded = jnp.pad(column_velocity, ((0, 0), (0, 0), (1, 1), (0, 0)))
    grad_z = (padded[:, :, 2:] - padded[:, :, :-2]) * 0.5
    columns = columns[3:6] - time_step * (column_velocity[2:3] * grad_z)
    solved = jnp.einsum("zk,cxky->cxzy", vertical_inverse, columns, precision=lax.Precision.HIGHEST)
    solved = solved.reshape(3, rows_x, rows_z, rows_y)
    new_velocity = lax.all_to_all(solved, "gx", split_axis=1, concat_axis=1, tiled=True)
    return new_velocity


def solution(mesh):
    placed = (
        P(None, "gy", "gx", None),
        P(None, ("gx", "gy")),
        P(("gx", "gy")),
        P(("gx", "gy")),
        P(("gx", "gy"), None),
        P(("gx", "gy"), None),
        P(None, ("gx", "gy"), None),
        P(("gx", "gy"), None),
        P(),
    )

    return jax.shard_map(
        local, mesh=mesh, in_specs=placed, out_specs=P(None, "gy", "gx", None), check_vma=False
    )
```
